32 devices in a mesh: groups: 2 (over y), freq: 4 (over z), tile: 4 (over x, core).
Axes of the slice: x: 2, y: 2, z: 4, core: 2. Of those that a mesh axis runs over, the one named last changes fastest.
Arguments:
- traces: bfloat16 [640, 32, 16384], P('freq', 'groups', 'tile'), parts along dimension 1, may hold values from -6 to 6
- v_factors: bfloat16 [4, 2, 32, 64, 8, 256], P('freq', None, None, 'tile'), may hold values from -0.375 to 0.375
- u_factors: bfloat16 [4, 2, 32, 64, 8, 256], P('freq', None, 'tile'), may hold values from -0.25 to 0.25
- ranks: int32 [4, 32, 64], P('freq', None, 'tile'), may hold values from 1 to 8
Outputs:
- convolved: bfloat16 [640, 32, 8192], P('freq', 'groups', 'tile'), parts along dimension 1
The draws below stay inside these ranges and needn't reach their ends.
There are 2 independent parts, one for each index of `groups`. The reference program is written for one: setup_inputs(seed, part) draws one part's arguments, and reference() takes and returns one part's arrays. A program takes and returns all parts, laid end to end along the dimension named above; an argument that names none is the same for every part. Nothing has to cross between parts.
All inputs are finite; a program needn't handle non-finite values.
Results may differ from the reference program's by a relative error of at most 0.0074.
Values may be sent and summed in bfloat16 or wider, within the bound.
No kernel may reach another device: no remote copies, remote signals or barrier semaphores. Data moves between devices by JAX's collectives and lax.ppermute only.
A program may use at most 192 MiB of HBM per device.

```python
import math
import jax
import jax.numpy as jnp
from jax import lax

TILE = 256
TC = 64
TR = 32
NT = 640
RMAX = 8
F0 = 40
NV = 16
NF = 4
NS = 16384
NR = 8192


def with_ends(drawn, key, low, high):
    dims = drawn.shape
    spot = [jax.random.randint(jax.random.fold_in(key, axis), (), 0, dims[axis]) for axis in range(len(dims))]
    drawn = drawn.at[tuple(spot)].set(low)
    longest = dims.index(max(dims))
    spot[longest] = (spot[longest] + 1) % dims[longest]
    return drawn.at[tuple(spot)].set(high)


def block_scale(rng, shape, split, least, top_value):
    loudness = 1.0
    for dim, parts in split:
        steps = jax.random.uniform(jax.random.fold_in(jax.random.fold_in(rng, 6), dim), (parts,), jnp.float32, least / len(split), top_value / len(split))
        loudness = loudness * jnp.repeat(jnp.exp(steps), shape[dim] // parts).reshape((-1,) + (1,) * (len(shape) - 1 - dim))
    return loudness


def normal_values(stream_key, dims, spread, bound, cuts=(), held_as=jnp.bfloat16):
    result = jax.random.normal(stream_key, dims, jnp.float32) * spread
    if len(cuts) > 0:
        result = block_scale(stream_key, dims, cuts, -0.22, 0.18) * result
    return jnp.clip(result, min=-bound, max=bound).astype(held_as)


def setup_inputs(seed: int = 0, part: int = 0) -> dict:
    key_list = jax.random.split(jax.random.key(seed), 5)
    part_splits = jax.random.split(jax.random.fold_in(key_list[4], part), 5)
    traces = normal_values(part_splits[0], (NT, NV, NS), 1.0, 6.0, ((0, 4), (2, 4)))
    v_factors = normal_values(key_list[1], (NF, 2, TR, TC, RMAX, TILE), TILE ** -0.5, 0.375, ((0, 4), (3, 4)))
    u_factors = normal_values(key_list[2], (NF, 2, TR, TC, RMAX, TILE), (TC * RMAX) ** -0.5, 0.25, ((0, 4), (2, 4)))
    ranks = with_ends(jax.random.randint(key_list[3], (NF, TR, TC), 1, RMAX + 1), jax.random.fold_in(key_list[3], 1), 1, RMAX).astype(jnp.int32)
    return dict(traces=traces, v_factors=v_factors, u_factors=u_factors, ranks=ranks)


def twiddle(freq_ids, time_ids):
    turns = (F0 + freq_ids)[:, None] * time_ids[None, :] % NT
    angle = turns.astype(jnp.float32) * (2.0 * math.pi / NT)
    return (jnp.cos(angle).astype(jnp.bfloat16), jnp.sin(angle).astype(jnp.bfloat16))

def source_side(operands):
    factors, spectrum_one, rank_one = operands
    wide = spectrum_one.reshape(2, NV, TC, TILE).astype(jnp.float32)
    factors_wide = factors.astype(jnp.float32)

    def product(left_operand_factors, right_operand_factors):
        return jnp.einsum('ajrs,vjs->ajrv', left_operand_factors, right_operand_factors)
    real_part = product(factors_wide[0], wide[0]) - product(factors_wide[1], wide[1])
    imag_part = product(factors_wide[0], wide[1]) + product(factors_wide[1], wide[0])
    rank_mask = jnp.arange(RMAX, dtype=jnp.int32)[None, None, :, None] < rank_one[:, :, None, None]
    stacked = jnp.stack([real_part, imag_part])
    return jnp.where(rank_mask[None], stacked, jnp.float32(0.0)).astype(jnp.bfloat16)

def receiver_side(operands):
    factors, coeffs = operands
    factors_wide = factors.astype(jnp.float32)
    coeffs_wide = coeffs.astype(jnp.float32)

    def product(left_operand_factors, right_operand_factors):
        return jnp.einsum('mdlh,mdlu->umh', left_operand_factors, right_operand_factors)
    real_part = product(factors_wide[0], coeffs_wide[0]) - product(factors_wide[1], coeffs_wide[1])
    imag_part = product(factors_wide[0], coeffs_wide[1]) + product(factors_wide[1], coeffs_wide[0])
    return jnp.stack([real_part, imag_part]).reshape(2, NV, NR).astype(jnp.bfloat16)

def reference(traces, v_factors, u_factors, ranks):
    freq_ids = jnp.arange(NF, dtype=jnp.int32)
    time_ids = jnp.arange(NT, dtype=jnp.int32)
    cosine, sine = twiddle(freq_ids, time_ids)
    flat_traces = traces.reshape(NT, NV * NS)
    real_part = jnp.dot(cosine, flat_traces, preferred_element_type=jnp.float32)
    imag_part = -jnp.dot(sine, flat_traces, preferred_element_type=jnp.float32)
    spectrum = (jnp.stack([real_part, imag_part], 1) * (1.0 / math.sqrt(NT))).astype(jnp.bfloat16)
    spectrum = spectrum.reshape(NF, 2, NV, NS)
    coefficients = lax.map(source_side, (v_factors, spectrum, ranks))
    received = lax.map(receiver_side, (u_factors, coefficients))
    real_flat = received[:, 0].reshape(NF, NV * NR)
    imag_flat = received[:, 1].reshape(NF, NV * NR)
    summed = jnp.dot(cosine.T, real_flat, preferred_element_type=jnp.float32) - jnp.dot(sine.T, imag_flat, preferred_element_type=jnp.float32)
    return (summed * (1.0 / math.sqrt(NF))).astype(jnp.bfloat16).reshape(NT, NV, NR)
```

```python
import math

import jax
import jax.numpy as jnp
from jax import lax
from jax.sharding import PartitionSpec as P

NT = 640
F0 = 40


def twiddle(freq_ids, time_ids):
    turns = (F0 + freq_ids)[:, None] * time_ids[None, :] % NT
    angle = turns.astype(jnp.float32) * (2.0 * math.pi / NT)
    return (jnp.cos(angle).astype(jnp.bfloat16), jnp.sin(angle).astype(jnp.bfloat16))


def spread_over(weights, count):
    eye = jnp.eye(count, dtype=weights.dtype)
    rows, cols = weights.shape
    return (weights[:, None, :, None] * eye[None, :, None, :]).reshape(rows * count, cols * count)


def per_device(traces, v_factors, u_factors, ranks):
    time_count = traces.shape[0]
    virtual_sources = traces.shape[1]
    source_count = traces.shape[2]
    freq_local = v_factors.shape[0]
    freq_total = freq_local * lax.axis_size("freq")
    tile_width = v_factors.shape[5]
    rank_positions = v_factors.shape[4]
    rows_all = v_factors.shape[2]
    columns = v_factors.shape[3]
    time_ids = lax.axis_index("freq") * time_count + jnp.arange(time_count, dtype=jnp.int32)
    scale_time = 1.0 / math.sqrt(NT)
    freq_ids = jnp.arange(freq_total, dtype=jnp.int32)
    cosine, sine = twiddle(freq_ids, time_ids)

    forward = jnp.stack([cosine, -sine], 1).reshape(freq_total * 2, time_count)
    flat_traces = traces.reshape(time_count * virtual_sources, source_count)
    partial = jnp.dot(
        spread_over(forward, virtual_sources), flat_traces, preferred_element_type=jnp.float32
    ).reshape(freq_total, 2, virtual_sources, source_count)
    summed = lax.psum_scatter(partial, "freq", scatter_dimension=0, tiled=True)
    spectrum = (summed * scale_time).astype(jnp.bfloat16)[0]
    spectral_tiles = spectrum.reshape(2, virtual_sources, columns, tile_width)
    emitter_factors = v_factors[0]

    def source_product(left_operand_factors, right_operand_factors):
        return jnp.einsum(
            "ajrs,vjs->ajrv",
            left_operand_factors,
            right_operand_factors,
            preferred_element_type=jnp.float32,
        )

    real_coeff = source_product(emitter_factors[0], spectral_tiles[0]) - source_product(
        emitter_factors[1], spectral_tiles[1]
    )
    imag_coeff = source_product(emitter_factors[0], spectral_tiles[1]) + source_product(
        emitter_factors[1], spectral_tiles[0]
    )
    rank_mask = (
        jnp.arange(rank_positions, dtype=jnp.int32)[None, None, :, None]
        < ranks[0][:, :, None, None]
    )
    stacked = jnp.stack([real_coeff, imag_coeff])
    coefficients = jnp.where(rank_mask[None], stacked, jnp.float32(0.0)).astype(jnp.bfloat16)
    coefficients = coefficients.reshape(2, rows_all, columns, rank_positions * virtual_sources)
    arrived = lax.all_to_all(coefficients, "tile", split_axis=1, concat_axis=2, tiled=True)
    rows_local = arrived.shape[1]
    columns_all = arrived.shape[2]
    arrived = arrived.reshape(2, rows_local, columns_all, rank_positions, virtual_sources)
    receiver_factors = u_factors[0]

    def receiver_product(left_operand_factors, right_operand_factors):
        return jnp.einsum(
            "mdlh,mdlu->umh",
            left_operand_factors,
            right_operand_factors,
            preferred_element_type=jnp.float32,
        )

    real_recv = receiver_product(receiver_factors[0], arrived[0]) - receiver_product(
        receiver_factors[1], arrived[1]
    )
    imag_recv = receiver_product(receiver_factors[0], arrived[1]) + receiver_product(
        receiver_factors[1], arrived[0]
    )
    receivers = rows_local * tile_width
    received = (
        jnp.stack([real_recv, imag_recv])
        .reshape(1, 2, virtual_sources, receivers)
        .astype(jnp.bfloat16)
    )
    piece = lax.all_gather(received, "freq", axis=0, tiled=True)
    count = piece.shape[0]

    backward = jnp.stack([cosine.T, -sine.T], 2).reshape(time_count, count * 2)
    added = jnp.dot(
        spread_over(backward, virtual_sources),
        piece.reshape(count * 2 * virtual_sources, receivers),
        preferred_element_type=jnp.float32,
    )
    scale_freq = 1.0 / math.sqrt(freq_total)
    return (added * scale_freq).astype(jnp.bfloat16).reshape(time_count, virtual_sources, receivers)


def solution(mesh):
    placed = (
        P("freq", "groups", "tile"),
        P("freq", None, None, "tile", None, None),
        P("freq", None, "tile", None, None, None),
        P("freq", None, "tile"),
    )
    return jax.shard_map(
        per_device,
        mesh=mesh,
        in_specs=placed,
        out_specs=P("freq", "groups", "tile"),
        check_vma=False,
    )
```

```python
import math

import jax
import jax.numpy as jnp
from jax import lax
from jax.sharding import PartitionSpec as P

NT = 640
F0 = 40


def twiddle(freq_ids, time_ids):
    turns = (F0 + freq_ids)[:, None] * time_ids[None, :] % NT
    angle = turns.astype(jnp.float32) * (2.0 * math.pi / NT)
    return (jnp.cos(angle).astype(jnp.bfloat16), jnp.sin(angle).astype(jnp.bfloat16))


def spread_over(weights, count):
    rows, cols = weights.shape
    kind = weights.dtype
    repeat_rows = (
        jnp.arange(rows * count, dtype=jnp.int32)[:, None] // count
        == jnp.arange(rows, dtype=jnp.int32)[None, :]
    ).astype(kind)
    repeat_cols = (
        jnp.arange(cols, dtype=jnp.int32)[:, None]
        == jnp.arange(cols * count, dtype=jnp.int32)[None, :] // count
    ).astype(kind)
    tall = jnp.dot(repeat_rows, weights, preferred_element_type=jnp.float32).astype(kind)
    wide = jnp.dot(tall, repeat_cols, preferred_element_type=jnp.float32)
    same = (
        jnp.arange(rows * count, dtype=jnp.int32)[:, None] % count
        == jnp.arange(cols * count, dtype=jnp.int32)[None, :] % count
    )
    return jnp.where(same, wide, jnp.float32(0.0)).astype(kind)


def per_device(traces, v_factors, u_factors, ranks):
    time_count = traces.shape[0]
    virtual_sources = traces.shape[1]
    source_count = traces.shape[2]
    freq_local = v_factors.shape[0]
    freq_total = freq_local * lax.axis_size("freq")
    tile_width = v_factors.shape[5]
    rank_positions = v_factors.shape[4]
    rows_all = v_factors.shape[2]
    columns = v_factors.shape[3]
    time_ids = lax.axis_index("freq") * time_count + jnp.arange(time_count, dtype=jnp.int32)
    scale_time = 1.0 / math.sqrt(NT)
    freq_ids = jnp.arange(freq_total, dtype=jnp.int32)
    cosine, sine = twiddle(freq_ids, time_ids)

    forward = jnp.stack([cosine, -sine], 1).reshape(freq_total * 2, time_count)
    flat_traces = traces.reshape(time_count * virtual_sources, source_count)
    partial = jnp.dot(
        spread_over(forward, virtual_sources), flat_traces, preferred_element_type=jnp.float32
    )
    partial = (partial * scale_time).astype(jnp.bfloat16)
    partial = partial.reshape(freq_total, 2, virtual_sources, source_count)
    spectrum = lax.psum_scatter(partial, "freq", scatter_dimension=0, tiled=True)[0]
    spectral_tiles = spectrum.reshape(2, virtual_sources, columns, tile_width)
    emitter_factors = v_factors[0]

    def source_product(left_operand_factors, right_operand_factors):
        return jnp.einsum(
            "ajrs,vjs->ajrv",
            left_operand_factors,
            right_operand_factors,
            preferred_element_type=jnp.float32,
        )

    real_coeff = source_product(emitter_factors[0], spectral_tiles[0]) - source_product(
        emitter_factors[1], spectral_tiles[1]
    )
    imag_coeff = source_product(emitter_factors[0], spectral_tiles[1]) + source_product(
        emitter_factors[1], spectral_tiles[0]
    )
    rank_mask = (
        jnp.arange(rank_positions, dtype=jnp.int32)[None, None, :, None]
        < ranks[0][:, :, None, None]
    )
    stacked = jnp.stack([real_coeff, imag_coeff])
    coefficients = jnp.where(rank_mask[None], stacked, jnp.float32(0.0)).astype(jnp.bfloat16)
    coefficients = coefficients.reshape(2, rows_all, columns, rank_positions * virtual_sources)
    arrived = lax.all_to_all(coefficients, "tile", split_axis=1, concat_axis=2, tiled=True)
    rows_local = arrived.shape[1]
    columns_all = arrived.shape[2]
    arrived = arrived.reshape(2, rows_local, columns_all, rank_positions, virtual_sources)
    receiver_factors = u_factors[0]

    def receiver_product(left_operand_factors, right_operand_factors):
        return jnp.einsum(
            "mdlh,mdlu->umh",
            left_operand_factors,
            right_operand_factors,
            preferred_element_type=jnp.float32,
        )

    real_recv = receiver_product(receiver_factors[0], arrived[0]) - receiver_product(
        receiver_factors[1], arrived[1]
    )
    imag_recv = receiver_product(receiver_factors[0], arrived[1]) + receiver_product(
        receiver_factors[1], arrived[0]
    )
    receivers = rows_local * tile_width
    received = (
        jnp.stack([real_recv, imag_recv])
        .reshape(1, 2, virtual_sources, receivers)
        .astype(jnp.bfloat16)
    )
    piece = lax.all_gather(received, "freq", axis=0, tiled=True)
    count = piece.shape[0]

    backward = jnp.stack([cosine.T, -sine.T], 2).reshape(time_count, count * 2)
    added = jnp.dot(
        spread_over(backward, virtual_sources),
        piece.reshape(count * 2 * virtual_sources, receivers),
        preferred_element_type=jnp.float32,
    )
    scale_freq = 1.0 / math.sqrt(freq_total)
    return (added * scale_freq).astype(jnp.bfloat16).reshape(time_count, virtual_sources, receivers)


def solution(mesh):
    placed = (
        P("freq", "groups", "tile"),
        P("freq", None, None, "tile", None, None),
        P("freq", None, "tile", None, None, None),
        P("freq", None, "tile"),
    )
    return jax.shard_map(
        per_device,
        mesh=mesh,
        in_specs=placed,
        out_specs=P("freq", "groups", "tile"),
        check_vma=False,
    )
```

```python
import math

import jax
import jax.numpy as jnp
from jax import lax
from jax.sharding import PartitionSpec as P

NT = 640
F0 = 40


def twiddle(freq_ids, time_ids):
    turns = (F0 + freq_ids)[:, None] * time_ids[None, :] % NT
    angle = turns.astype(jnp.float32) * (2.0 * math.pi / NT)
    return (jnp.cos(angle).astype(jnp.bfloat16), jnp.sin(angle).astype(jnp.bfloat16))


def spread_over(weights, count):
    rows, cols = weights.shape
    kind = weights.dtype
    repeat_rows = (
        jnp.arange(rows * count, dtype=jnp.int32)[:, None] // count
        == jnp.arange(rows, dtype=jnp.int32)[None, :]
    ).astype(kind)
    repeat_cols = (
        jnp.arange(cols, dtype=jnp.int32)[:, None]
        == jnp.arange(cols * count, dtype=jnp.int32)[None, :] // count
    ).astype(kind)
    tall = jnp.dot(repeat_rows, weights, preferred_element_type=jnp.float32).astype(kind)
    wide = jnp.dot(tall, repeat_cols, preferred_element_type=jnp.float32)
    same = (
        jnp.arange(rows * count, dtype=jnp.int32)[:, None] % count
        == jnp.arange(cols * count, dtype=jnp.int32)[None, :] % count
    )
    return jnp.where(same, wide, jnp.float32(0.0)).astype(kind)


def line_reduce_scatter(partial, axis):
    count = partial.shape[0]
    own = lax.axis_index(axis)

    def block(index):
        return lax.dynamic_index_in_dim(partial, jnp.clip(index, 0, count - 1), 0, keepdims=False)

    right = jnp.zeros_like(partial[0])
    left = jnp.zeros_like(partial[0])
    for step in range(1, count):
        send_right = block(count - step + own) + right
        send_left = block(own + step - count) + left
        right = lax.ppermute(send_right, axis, [(p, p + 1) for p in range(step)])
        left = lax.ppermute(send_left, axis, [(count - 1 - p, count - 2 - p) for p in range(step)])
    return block(own) + right + left


def line_all_gather(piece, axis, count):
    own = lax.axis_index(axis)
    slots = jnp.zeros((count,) + piece.shape, piece.dtype)
    slots = lax.dynamic_update_index_in_dim(slots, piece, own, 0)
    right = piece
    left = piece
    for step in range(1, count):
        right = lax.ppermute(right, axis, [(p, p + 1) for p in range(step - 1, count - 1)])
        left = lax.ppermute(left, axis, [(p + 1, p) for p in range(0, count - step)])
        for arrived, origin, valid in (
            (right, own - step, own >= step),
            (left, own + step, own + step <= count - 1),
        ):
            index = jnp.clip(origin, 0, count - 1)
            current = lax.dynamic_index_in_dim(slots, index, 0, keepdims=False)
            slots = lax.dynamic_update_index_in_dim(
                slots, jnp.where(valid, arrived, current), index, 0
            )
    return slots


def per_device(traces, v_factors, u_factors, ranks):
    time_count = traces.shape[0]
    virtual_sources = traces.shape[1]
    source_count = traces.shape[2]
    freq_local = v_factors.shape[0]
    freq_total = freq_local * lax.axis_size("freq")
    tile_width = v_factors.shape[5]
    rank_positions = v_factors.shape[4]
    rows_all = v_factors.shape[2]
    columns = v_factors.shape[3]
    time_ids = lax.axis_index("freq") * time_count + jnp.arange(time_count, dtype=jnp.int32)
    scale_time = 1.0 / math.sqrt(NT)
    freq_ids = jnp.arange(freq_total, dtype=jnp.int32)
    cosine, sine = twiddle(freq_ids, time_ids)

    forward = jnp.stack([cosine, -sine], 1).reshape(freq_total * 2, time_count)
    flat_traces = traces.reshape(time_count * virtual_sources, source_count)
    partial = jnp.dot(
        spread_over(forward, virtual_sources), flat_traces, preferred_element_type=jnp.float32
    ).reshape(freq_total, 2, virtual_sources, source_count)
    summed = line_reduce_scatter(partial, "freq")
    spectrum = (summed * scale_time).astype(jnp.bfloat16)
    spectral_tiles = spectrum.reshape(2, virtual_sources, columns, tile_width)
    emitter_factors = v_factors[0]

    def source_product(left_operand_factors, right_operand_factors):
        return jnp.einsum(
            "ajrs,vjs->ajrv",
            left_operand_factors,
            right_operand_factors,
            preferred_element_type=jnp.float32,
        )

    real_coeff = source_product(emitter_factors[0], spectral_tiles[0]) - source_product(
        emitter_factors[1], spectral_tiles[1]
    )
    imag_coeff = source_product(emitter_factors[0], spectral_tiles[1]) + source_product(
        emitter_factors[1], spectral_tiles[0]
    )
    rank_mask = (
        jnp.arange(rank_positions, dtype=jnp.int32)[None, None, :, None]
        < ranks[0][:, :, None, None]
    )
    stacked = jnp.stack([real_coeff, imag_coeff])
    coefficients = jnp.where(rank_mask[None], stacked, jnp.float32(0.0)).astype(jnp.bfloat16)
    coefficients = coefficients.reshape(2, rows_all, columns, rank_positions * virtual_sources)
    arrived = lax.all_to_all(coefficients, "tile", split_axis=1, concat_axis=2, tiled=True)
    rows_local = arrived.shape[1]
    columns_all = arrived.shape[2]
    arrived = arrived.reshape(2, rows_local, columns_all, rank_positions, virtual_sources)
    receiver_factors = u_factors[0]

    def receiver_product(left_operand_factors, right_operand_factors):
        return jnp.einsum(
            "mdlh,mdlu->umh",
            left_operand_factors,
            right_operand_factors,
            preferred_element_type=jnp.float32,
        )

    real_recv = receiver_product(receiver_factors[0], arrived[0]) - receiver_product(
        receiver_factors[1], arrived[1]
    )
    imag_recv = receiver_product(receiver_factors[0], arrived[1]) + receiver_product(
        receiver_factors[1], arrived[0]
    )
    receivers = rows_local * tile_width
    received = (
        jnp.stack([real_recv, imag_recv])
        .reshape(1, 2, virtual_sources, receivers)
        .astype(jnp.bfloat16)
    )
    count = freq_total
    piece = line_all_gather(received[0], "freq", count)

    backward = jnp.stack([cosine.T, -sine.T], 2).reshape(time_count, count * 2)
    added = jnp.dot(
        spread_over(backward, virtual_sources),
        piece.reshape(count * 2 * virtual_sources, receivers),
        preferred_element_type=jnp.float32,
    )
    scale_freq = 1.0 / math.sqrt(freq_total)
    return (added * scale_freq).astype(jnp.bfloat16).reshape(time_count, virtual_sources, receivers)


def solution(mesh):
    placed = (
        P("freq", "groups", "tile"),
        P("freq", None, None, "tile", None, None),
        P("freq", None, "tile", None, None, None),
        P("freq", None, "tile"),
    )
    return jax.shard_map(
        per_device,
        mesh=mesh,
        in_specs=placed,
        out_specs=P("freq", "groups", "tile"),
        check_vma=False,
    )
```

```python
import math

import jax
import jax.numpy as jnp
from jax import lax
from jax.sharding import PartitionSpec as P

NT = 640
F0 = 40
CHUNKS = 2


def twiddle(freq_ids, time_ids):
    turns = (F0 + freq_ids)[:, None] * time_ids[None, :] % NT
    angle = turns.astype(jnp.float32) * (2.0 * math.pi / NT)
    return (jnp.cos(angle).astype(jnp.bfloat16), jnp.sin(angle).astype(jnp.bfloat16))


def spread_over(weights, count):
    rows, cols = weights.shape
    kind = weights.dtype
    repeat_rows = (
        jnp.arange(rows * count, dtype=jnp.int32)[:, None] // count
        == jnp.arange(rows, dtype=jnp.int32)[None, :]
    ).astype(kind)
    repeat_cols = (
        jnp.arange(cols, dtype=jnp.int32)[:, None]
        == jnp.arange(cols * count, dtype=jnp.int32)[None, :] // count
    ).astype(kind)
    tall = jnp.dot(repeat_rows, weights, preferred_element_type=jnp.float32).astype(kind)
    wide = jnp.dot(tall, repeat_cols, preferred_element_type=jnp.float32)
    same = (
        jnp.arange(rows * count, dtype=jnp.int32)[:, None] % count
        == jnp.arange(cols * count, dtype=jnp.int32)[None, :] % count
    )
    return jnp.where(same, wide, jnp.float32(0.0)).astype(kind)


def per_device(traces, v_factors, u_factors, ranks):
    time_count = traces.shape[0]
    virtual_sources = traces.shape[1]
    source_count = traces.shape[2]
    freq_local = v_factors.shape[0]
    freq_total = freq_local * lax.axis_size("freq")
    tile_width = v_factors.shape[5]
    rank_positions = v_factors.shape[4]
    rows_all = v_factors.shape[2]
    columns = v_factors.shape[3]
    time_ids = lax.axis_index("freq") * time_count + jnp.arange(time_count, dtype=jnp.int32)
    scale_time = 1.0 / math.sqrt(NT)
    freq_ids = jnp.arange(freq_total, dtype=jnp.int32)
    cosine, sine = twiddle(freq_ids, time_ids)
    chunks = CHUNKS if virtual_sources % CHUNKS == 0 else 1
    width = virtual_sources // chunks

    forward = spread_over(
        jnp.stack([cosine, -sine], 1).reshape(freq_total * 2, time_count), width
    )
    emitter_factors = v_factors[0]
    receiver_factors = u_factors[0]
    rank_mask = (
        jnp.arange(rank_positions, dtype=jnp.int32)[None, None, :, None]
        < ranks[0][:, :, None, None]
    )

    def source_product(left_operand_factors, right_operand_factors):
        return jnp.einsum(
            "ajrs,vjs->ajrv",
            left_operand_factors,
            right_operand_factors,
            preferred_element_type=jnp.float32,
        )

    def receiver_product(left_operand_factors, right_operand_factors):
        return jnp.einsum(
            "mdlh,mdlu->umh",
            left_operand_factors,
            right_operand_factors,
            preferred_element_type=jnp.float32,
        )

    sums = []
    for part in range(chunks):
        flat_traces = traces[:, part * width:(part + 1) * width, :].reshape(
            time_count * width, source_count
        )
        partial = jnp.dot(forward, flat_traces, preferred_element_type=jnp.float32).reshape(
            freq_total, 2, width, source_count
        )
        sums.append(lax.psum_scatter(partial, "freq", scatter_dimension=0, tiled=True))
    pieces = []
    for part in range(chunks):
        summed = sums[part]
        if pieces:
            summed, pieces[-1] = lax.optimization_barrier((summed, pieces[-1]))
        spectrum = (summed * scale_time).astype(jnp.bfloat16)[0]
        spectral_tiles = spectrum.reshape(2, width, columns, tile_width)
        real_coeff = source_product(emitter_factors[0], spectral_tiles[0]) - source_product(
            emitter_factors[1], spectral_tiles[1]
        )
        imag_coeff = source_product(emitter_factors[0], spectral_tiles[1]) + source_product(
            emitter_factors[1], spectral_tiles[0]
        )
        stacked = jnp.stack([real_coeff, imag_coeff])
        coefficients = jnp.where(rank_mask[None], stacked, jnp.float32(0.0)).astype(jnp.bfloat16)
        coefficients = coefficients.reshape(2, rows_all, columns, rank_positions * width)
        arrived = lax.all_to_all(coefficients, "tile", split_axis=1, concat_axis=2, tiled=True)
        rows_local = arrived.shape[1]
        columns_all = arrived.shape[2]
        arrived = arrived.reshape(2, rows_local, columns_all, rank_positions, width)
        real_recv = receiver_product(receiver_factors[0], arrived[0]) - receiver_product(
            receiver_factors[1], arrived[1]
        )
        imag_recv = receiver_product(receiver_factors[0], arrived[1]) + receiver_product(
            receiver_factors[1], arrived[0]
        )
        receivers = rows_local * tile_width
        received = (
            jnp.stack([real_recv, imag_recv])
            .reshape(1, 2, width, receivers)
            .astype(jnp.bfloat16)
        )
        pieces.append(lax.all_gather(received, "freq", axis=0, tiled=True))
    piece = jnp.concatenate(pieces, axis=2)
    count = piece.shape[0]

    backward = jnp.stack([cosine.T, -sine.T], 2).reshape(time_count, count * 2)
    added = jnp.dot(
        spread_over(backward, virtual_sources),
        piece.reshape(count * 2 * virtual_sources, receivers),
        preferred_element_type=jnp.float32,
    )
    scale_freq = 1.0 / math.sqrt(freq_total)
    return (added * scale_freq).astype(jnp.bfloat16).reshape(time_count, virtual_sources, receivers)


def solution(mesh):
    placed = (
        P("freq", "groups", "tile"),
        P("freq", None, None, "tile", None, None),
        P("freq", None, "tile", None, None, None),
        P("freq", None, "tile"),
    )
    return jax.shard_map(
        per_device,
        mesh=mesh,
        in_specs=placed,
        out_specs=P("freq", "groups", "tile"),
        check_vma=False,
    )
```

```python
import math

import jax
import jax.numpy as jnp
from jax import lax
from jax.sharding import PartitionSpec as P

NT = 640
F0 = 40


def twiddle(freq_ids, time_ids):
    turns = (F0 + freq_ids)[:, None] * time_ids[None, :] % NT
    angle = turns.astype(jnp.float32) * (2.0 * math.pi / NT)
    return (jnp.cos(angle).astype(jnp.bfloat16), jnp.sin(angle).astype(jnp.bfloat16))


def spread_over(weights, count):
    rows, cols = weights.shape
    kind = weights.dtype
    repeat_rows = (
        jnp.arange(rows * count, dtype=jnp.int32)[:, None] // count
        == jnp.arange(rows, dtype=jnp.int32)[None, :]
    ).astype(kind)
    repeat_cols = (
        jnp.arange(cols, dtype=jnp.int32)[:, None]
        == jnp.arange(cols * count, dtype=jnp.int32)[None, :] // count
    ).astype(kind)
    tall = jnp.dot(repeat_rows, weights, preferred_element_type=jnp.float32).astype(kind)
    wide = jnp.dot(tall, repeat_cols, preferred_element_type=jnp.float32)
    same = (
        jnp.arange(rows * count, dtype=jnp.int32)[:, None] % count
        == jnp.arange(cols * count, dtype=jnp.int32)[None, :] % count
    )
    return jnp.where(same, wide, jnp.float32(0.0)).astype(kind)


def per_device(traces, v_factors, u_factors, ranks):
    time_count = traces.shape[0]
    virtual_sources = traces.shape[1]
    source_count = traces.shape[2]
    freq_local = v_factors.shape[0]
    freq_total = freq_local * lax.axis_size("freq")
    tile_width = v_factors.shape[5]
    rank_positions = v_factors.shape[4]
    rows_all = v_factors.shape[2]
    columns = v_factors.shape[3]
    time_ids = lax.axis_index("freq") * time_count + jnp.arange(time_count, dtype=jnp.int32)
    scale_time = 1.0 / math.sqrt(NT)
    freq_ids = jnp.arange(freq_total, dtype=jnp.int32)
    cosine, sine = twiddle(freq_ids, time_ids)

    forward = jnp.stack([cosine, -sine], 1).reshape(freq_total * 2, time_count)
    flat_traces = traces.reshape(time_count * virtual_sources, source_count)
    partial = jnp.dot(
        spread_over(forward, virtual_sources), flat_traces, preferred_element_type=jnp.float32
    ).reshape(freq_total, 2, virtual_sources, source_count)
    summed = lax.psum_scatter(partial, "freq", scatter_dimension=0, tiled=True)
    spectrum = (summed * scale_time).astype(jnp.bfloat16)[0]
    spectral_tiles = spectrum.reshape(2, virtual_sources, columns, tile_width)
    emitter_factors = v_factors[0]
    real_part, imag_part = spectral_tiles[0], spectral_tiles[1]
    stacked_spectrum = jnp.stack(
        [jnp.stack([real_part, -imag_part]), jnp.stack([imag_part, real_part])]
    )
    stacked = jnp.einsum(
        "iajrs,oivjs->oajrv",
        emitter_factors,
        stacked_spectrum,
        preferred_element_type=jnp.float32,
    )
    rank_mask = (
        jnp.arange(rank_positions, dtype=jnp.int32)[None, None, :, None]
        < ranks[0][:, :, None, None]
    )
    coefficients = jnp.where(rank_mask[None], stacked, jnp.float32(0.0)).astype(jnp.bfloat16)
    coefficients = coefficients.reshape(2, rows_all, columns, rank_positions * virtual_sources)
    arrived = lax.all_to_all(coefficients, "tile", split_axis=1, concat_axis=2, tiled=True)
    rows_local = arrived.shape[1]
    columns_all = arrived.shape[2]
    arrived = arrived.reshape(2, rows_local, columns_all, rank_positions, virtual_sources)
    receiver_factors = u_factors[0]
    real_arrived, imag_arrived = arrived[0], arrived[1]
    stacked_arrived = jnp.stack(
        [jnp.stack([real_arrived, -imag_arrived]), jnp.stack([imag_arrived, real_arrived])]
    )
    receivers = rows_local * tile_width
    received = (
        jnp.einsum(
            "imdlh,oimdlu->oumh",
            receiver_factors,
            stacked_arrived,
            preferred_element_type=jnp.float32,
        )
        .reshape(1, 2, virtual_sources, receivers)
        .astype(jnp.bfloat16)
    )
    piece = lax.all_gather(received, "freq", axis=0, tiled=True)
    count = piece.shape[0]

    backward = jnp.stack([cosine.T, -sine.T], 2).reshape(time_count, count * 2)
    added = jnp.dot(
        spread_over(backward, virtual_sources),
        piece.reshape(count * 2 * virtual_sources, receivers),
        preferred_element_type=jnp.float32,
    )
    scale_freq = 1.0 / math.sqrt(freq_total)
    return (added * scale_freq).astype(jnp.bfloat16).reshape(time_count, virtual_sources, receivers)


def solution(mesh):
    placed = (
        P("freq", "groups", "tile"),
        P("freq", None, None, "tile", None, None),
        P("freq", None, "tile", None, None, None),
        P("freq", None, "tile"),
    )
    return jax.shard_map(
        per_device,
        mesh=mesh,
        in_specs=placed,
        out_specs=P("freq", "groups", "tile"),
        check_vma=False,
    )
```

```python
import math

import jax
import jax.numpy as jnp
from jax import lax
from jax.sharding import PartitionSpec as P

NT = 640
F0 = 40


def twiddle(freq_ids, time_ids):
    turns = (F0 + freq_ids)[:, None] * time_ids[None, :] % NT
    angle = turns.astype(jnp.float32) * (2.0 * math.pi / NT)
    return (jnp.cos(angle).astype(jnp.bfloat16), jnp.sin(angle).astype(jnp.bfloat16))


def spread_over(weights, count):
    rows, cols = weights.shape
    kind = weights.dtype
    repeat_rows = (
        jnp.arange(rows * count, dtype=jnp.int32)[:, None] // count
        == jnp.arange(rows, dtype=jnp.int32)[None, :]
    ).astype(kind)
    repeat_cols = (
        jnp.arange(cols, dtype=jnp.int32)[:, None]
        == jnp.arange(cols * count, dtype=jnp.int32)[None, :] // count
    ).astype(kind)
    tall = jnp.dot(repeat_rows, weights, preferred_element_type=jnp.float32).astype(kind)
    wide = jnp.dot(tall, repeat_cols, preferred_element_type=jnp.float32)
    same = (
        jnp.arange(rows * count, dtype=jnp.int32)[:, None] % count
        == jnp.arange(cols * count, dtype=jnp.int32)[None, :] % count
    )
    return jnp.where(same, wide, jnp.float32(0.0)).astype(kind)


def per_device(traces, v_factors, u_factors, ranks):
    time_count = traces.shape[0]
    virtual_sources = traces.shape[1]
    source_count = traces.shape[2]
    freq_local = v_factors.shape[0]
    freq_total = freq_local * lax.axis_size("freq")
    tile_width = v_factors.shape[5]
    rank_positions = v_factors.shape[4]
    rows_all = v_factors.shape[2]
    columns = v_factors.shape[3]
    time_ids = lax.axis_index("freq") * time_count + jnp.arange(time_count, dtype=jnp.int32)
    scale_time = 1.0 / math.sqrt(NT)
    freq_ids = jnp.arange(freq_total, dtype=jnp.int32)
    cosine, sine = twiddle(freq_ids, time_ids)

    forward = jnp.stack([cosine, -sine], 1).reshape(freq_total * 2, time_count)
    flat_traces = traces.reshape(time_count * virtual_sources, source_count)
    partial = jnp.dot(
        spread_over(forward, virtual_sources), flat_traces, preferred_element_type=jnp.float32
    ).reshape(freq_total, 2, virtual_sources, source_count)
    gathered = lax.all_to_all(partial, "freq", split_axis=0, concat_axis=0, tiled=True)
    summed = gathered.reshape(
        lax.axis_size("freq"), freq_local, 2, virtual_sources, source_count
    ).sum(axis=0)
    spectrum = (summed * scale_time).astype(jnp.bfloat16)[0]
    spectral_tiles = spectrum.reshape(2, virtual_sources, columns, tile_width)
    emitter_factors = v_factors[0]
    real_part, imag_part = spectral_tiles[0], spectral_tiles[1]
    stacked_spectrum = jnp.stack(
        [jnp.stack([real_part, -imag_part]), jnp.stack([imag_part, real_part])]
    )
    stacked = jnp.einsum(
        "iajrs,oivjs->oajrv",
        emitter_factors,
        stacked_spectrum,
        preferred_element_type=jnp.float32,
    )
    rank_mask = (
        jnp.arange(rank_positions, dtype=jnp.int32)[None, None, :, None]
        < ranks[0][:, :, None, None]
    )
    coefficients = jnp.where(rank_mask[None], stacked, jnp.float32(0.0)).astype(jnp.bfloat16)
    coefficients = coefficients.reshape(2, rows_all, columns, rank_positions * virtual_sources)
    arrived = lax.all_to_all(coefficients, "tile", split_axis=1, concat_axis=2, tiled=True)
    rows_local = arrived.shape[1]
    columns_all = arrived.shape[2]
    arrived = arrived.reshape(2, rows_local, columns_all, rank_positions, virtual_sources)
    receiver_factors = u_factors[0]
    real_arrived, imag_arrived = arrived[0], arrived[1]
    stacked_arrived = jnp.stack(
        [jnp.stack([real_arrived, -imag_arrived]), jnp.stack([imag_arrived, real_arrived])]
    )
    receivers = rows_local * tile_width
    received = (
        jnp.einsum(
            "imdlh,oimdlu->oumh",
            receiver_factors,
            stacked_arrived,
            preferred_element_type=jnp.float32,
        )
        .reshape(1, 2, virtual_sources, receivers)
        .astype(jnp.bfloat16)
    )
    piece = lax.all_gather(received, "freq", axis=0, tiled=True)
    count = piece.shape[0]

    backward = jnp.stack([cosine.T, -sine.T], 2).reshape(time_count, count * 2)
    added = jnp.dot(
        spread_over(backward, virtual_sources),
        piece.reshape(count * 2 * virtual_sources, receivers),
        preferred_element_type=jnp.float32,
    )
    scale_freq = 1.0 / math.sqrt(freq_total)
    return (added * scale_freq).astype(jnp.bfloat16).reshape(time_count, virtual_sources, receivers)


def solution(mesh):
    placed = (
        P("freq", "groups", "tile"),
        P("freq", None, None, "tile", None, None),
        P("freq", None, "tile", None, None, None),
        P("freq", None, "tile"),
    )
    return jax.shard_map(
        per_device,
        mesh=mesh,
        in_specs=placed,
        out_specs=P("freq", "groups", "tile"),
        check_vma=False,
    )
```

```python
import math

import jax
import jax.numpy as jnp
from jax import lax
from jax.sharding import PartitionSpec as P

NT = 640
F0 = 40


def twiddle(freq_ids, time_ids):
    turns = (F0 + freq_ids)[:, None] * time_ids[None, :] % NT
    angle = turns.astype(jnp.float32) * (2.0 * math.pi / NT)
    return (jnp.cos(angle).astype(jnp.bfloat16), jnp.sin(angle).astype(jnp.bfloat16))


def spread_over(weights, count):
    rows, cols = weights.shape
    kind = weights.dtype
    repeat_rows = (
        jnp.arange(rows * count, dtype=jnp.int32)[:, None] // count
        == jnp.arange(rows, dtype=jnp.int32)[None, :]
    ).astype(kind)
    repeat_cols = (
        jnp.arange(cols, dtype=jnp.int32)[:, None]
        == jnp.arange(cols * count, dtype=jnp.int32)[None, :] // count
    ).astype(kind)
    tall = jnp.dot(repeat_rows, weights, preferred_element_type=jnp.float32).astype(kind)
    wide = jnp.dot(tall, repeat_cols, preferred_element_type=jnp.float32)
    same = (
        jnp.arange(rows * count, dtype=jnp.int32)[:, None] % count
        == jnp.arange(cols * count, dtype=jnp.int32)[None, :] % count
    )
    return jnp.where(same, wide, jnp.float32(0.0)).astype(kind)


def per_device(traces, v_factors, u_factors, ranks):
    time_count = traces.shape[0]
    virtual_sources = traces.shape[1]
    source_count = traces.shape[2]
    freq_local = v_factors.shape[0]
    freq_total = freq_local * lax.axis_size("freq")
    tile_width = v_factors.shape[5]
    rank_positions = v_factors.shape[4]
    rows_all = v_factors.shape[2]
    columns = v_factors.shape[3]
    time_ids = lax.axis_index("freq") * time_count + jnp.arange(time_count, dtype=jnp.int32)
    scale_time = 1.0 / math.sqrt(NT)
    freq_ids = jnp.arange(freq_total, dtype=jnp.int32)
    cosine, sine = twiddle(freq_ids, time_ids)

    forward = jnp.stack([cosine, -sine], 1).reshape(freq_total * 2, time_count)
    flat_traces = traces.reshape(time_count * virtual_sources, source_count)
    partial = jnp.dot(
        spread_over(forward, virtual_sources), flat_traces, preferred_element_type=jnp.float32
    ).reshape(freq_total, 2, virtual_sources, source_count)
    gathered = lax.all_to_all(partial, "freq", split_axis=0, concat_axis=0, tiled=True)
    tile_count = lax.axis_size("tile")
    rows_local = rows_all // tile_count
    emitter_factors = jnp.transpose(v_factors[0], (2, 1, 3, 0, 4))
    receiver_factors = jnp.transpose(
        u_factors[0].reshape(2, rows_local, tile_count, columns, rank_positions, tile_width),
        (1, 2, 0, 3, 4, 5),
    )
    gathered, emitter_factors, receiver_factors = lax.optimization_barrier(
        (gathered, emitter_factors, receiver_factors)
    )
    summed = gathered.reshape(
        lax.axis_size("freq"), freq_local, 2, virtual_sources, source_count
    ).sum(axis=0)
    spectrum = (summed * scale_time).astype(jnp.bfloat16)[0]
    spectral_tiles = spectrum.reshape(2, virtual_sources, columns, tile_width)
    real_part, imag_part = spectral_tiles[0], spectral_tiles[1]
    stacked_spectrum = jnp.stack(
        [jnp.stack([real_part, -imag_part]), jnp.stack([imag_part, real_part])]
    )
    stacked = jnp.einsum(
        "jaris,oivjs->aojrv",
        emitter_factors,
        stacked_spectrum,
        preferred_element_type=jnp.float32,
    )
    rank_mask = (
        jnp.arange(rank_positions, dtype=jnp.int32)[None, None, :, None]
        < ranks[0][:, :, None, None]
    )
    coefficients = jnp.where(rank_mask[:, None], stacked, jnp.float32(0.0)).astype(jnp.bfloat16)
    coefficients = coefficients.reshape(
        tile_count, rows_local, 2, columns, rank_positions * virtual_sources
    )
    arrived = lax.all_to_all(coefficients, "tile", split_axis=0, concat_axis=0, tiled=True)
    arrived = arrived.reshape(
        tile_count, rows_local, 2, columns, rank_positions, virtual_sources
    )
    real_arrived, imag_arrived = arrived[:, :, 0], arrived[:, :, 1]
    stacked_arrived = jnp.stack(
        [jnp.stack([real_arrived, -imag_arrived]), jnp.stack([imag_arrived, real_arrived])]
    )
    receivers = rows_local * tile_width
    received = (
        jnp.einsum(
            "apijrb,oipajrv->ovab",
            receiver_factors,
            stacked_arrived,
            preferred_element_type=jnp.float32,
        )
        .reshape(1, 2, virtual_sources, receivers)
        .astype(jnp.bfloat16)
    )
    piece = lax.all_gather(received, "freq", axis=0, tiled=True)
    count = piece.shape[0]

    backward = jnp.stack([cosine.T, -sine.T], 2).reshape(time_count, count * 2)
    added = jnp.dot(
        spread_over(backward, virtual_sources),
        piece.reshape(count * 2 * virtual_sources, receivers),
        preferred_element_type=jnp.float32,
    )
    scale_freq = 1.0 / math.sqrt(freq_total)
    return (added * scale_freq).astype(jnp.bfloat16).reshape(time_count, virtual_sources, receivers)


def solution(mesh):
    placed = (
        P("freq", "groups", "tile"),
        P("freq", None, None, "tile", None, None),
        P("freq", None, "tile", None, None, None),
        P("freq", None, "tile"),
    )
    return jax.shard_map(
        per_device,
        mesh=mesh,
        in_specs=placed,
        out_specs=P("freq", "groups", "tile"),
        check_vma=False,
    )
```

```python
import math

import functools

import jax
import jax.numpy as jnp
from jax import lax
from jax.experimental import pallas as pl
from jax.sharding import PartitionSpec as P

NT = 640
F0 = 40


def twiddle(freq_ids, time_ids):
    turns = (F0 + freq_ids)[:, None] * time_ids[None, :] % NT
    angle = turns.astype(jnp.float32) * (2.0 * math.pi / NT)
    return (jnp.cos(angle).astype(jnp.bfloat16), jnp.sin(angle).astype(jnp.bfloat16))


def spread_over(weights, count):
    rows, cols = weights.shape
    kind = weights.dtype
    repeat_rows = (
        jnp.arange(rows * count, dtype=jnp.int32)[:, None] // count
        == jnp.arange(rows, dtype=jnp.int32)[None, :]
    ).astype(kind)
    repeat_cols = (
        jnp.arange(cols, dtype=jnp.int32)[:, None]
        == jnp.arange(cols * count, dtype=jnp.int32)[None, :] // count
    ).astype(kind)
    tall = jnp.dot(repeat_rows, weights, preferred_element_type=jnp.float32).astype(kind)
    wide = jnp.dot(tall, repeat_cols, preferred_element_type=jnp.float32)
    same = (
        jnp.arange(rows * count, dtype=jnp.int32)[:, None] % count
        == jnp.arange(cols * count, dtype=jnp.int32)[None, :] % count
    )
    return jnp.where(same, wide, jnp.float32(0.0)).astype(kind)


def source_kernel(v_ref, x_ref, o_ref, *, group, tile_width, lhs_rows):
    for column in range(group):
        real_f = v_ref[0, :, column].astype(jnp.float32).reshape(lhs_rows, tile_width)
        imag_f = v_ref[1, :, column].astype(jnp.float32).reshape(lhs_rows, tile_width)
        lanes = slice(column * tile_width, (column + 1) * tile_width)
        real_x = x_ref[0, :, lanes].astype(jnp.float32)
        imag_x = x_ref[1, :, lanes].astype(jnp.float32)
        lhs = jnp.concatenate([real_f, imag_f], axis=1).astype(jnp.bfloat16)
        rhs = jnp.concatenate(
            [jnp.concatenate([real_x, -imag_x], axis=1), jnp.concatenate([imag_x, real_x], axis=1)],
            axis=0,
        ).astype(jnp.bfloat16)
        o_ref[column] = lax.dot_general(
            lhs, rhs, (((1,), (1,)), ((), ())), preferred_element_type=jnp.float32
        )

def source_side(factors, spectrum, interpret=False):
    _, rows, columns, ranks, tile_width = factors.shape
    virtual = spectrum.shape[1]
    group = 4 if columns % 4 == 0 else 1
    return pl.pallas_call(
        functools.partial(source_kernel, group=group, tile_width=tile_width, lhs_rows=rows * ranks),
        grid=(columns // group,),
        in_specs=[
            pl.BlockSpec((2, rows, group, ranks, tile_width), lambda g: (0, 0, g, 0, 0)),
            pl.BlockSpec((2, virtual, group * tile_width), lambda g: (0, 0, g)),
        ],
        out_specs=pl.BlockSpec((group, rows * ranks, 2 * virtual), lambda g: (g, 0, 0)),
        out_shape=jax.ShapeDtypeStruct((columns, rows * ranks, 2 * virtual), jnp.float32),
        interpret=interpret,
    )(factors, spectrum)


def per_device(traces, v_factors, u_factors, ranks):
    time_count = traces.shape[0]
    virtual_sources = traces.shape[1]
    source_count = traces.shape[2]
    freq_local = v_factors.shape[0]
    freq_total = freq_local * lax.axis_size("freq")
    tile_width = v_factors.shape[5]
    rank_positions = v_factors.shape[4]
    rows_all = v_factors.shape[2]
    columns = v_factors.shape[3]
    time_ids = lax.axis_index("freq") * time_count + jnp.arange(time_count, dtype=jnp.int32)
    scale_time = 1.0 / math.sqrt(NT)
    freq_ids = jnp.arange(freq_total, dtype=jnp.int32)
    cosine, sine = twiddle(freq_ids, time_ids)

    forward = jnp.stack([cosine, -sine], 1).reshape(freq_total * 2, time_count)
    flat_traces = traces.reshape(time_count * virtual_sources, source_count)
    partial = jnp.dot(
        spread_over(forward, virtual_sources), flat_traces, preferred_element_type=jnp.float32
    ).reshape(freq_total, 2, virtual_sources, source_count)
    gathered = lax.all_to_all(partial, "freq", split_axis=0, concat_axis=0, tiled=True)
    summed = gathered.reshape(
        lax.axis_size("freq"), freq_local, 2, virtual_sources, source_count
    ).sum(axis=0)
    spectrum = (summed * scale_time).astype(jnp.bfloat16)[0]
    raw = source_side(v_factors[0], spectrum).reshape(
        columns, rows_all, rank_positions, 2, virtual_sources
    )
    rank_mask = (
        jnp.arange(rank_positions, dtype=jnp.int32)[None, None, :]
        < jnp.transpose(ranks[0])[:, :, None]
    )
    coefficients = (
        jnp.where(rank_mask[:, :, :, None, None], raw, jnp.float32(0.0))
        .astype(jnp.bfloat16)
        .transpose(3, 1, 0, 2, 4)
    )
    coefficients = coefficients.reshape(2, rows_all, columns, rank_positions * virtual_sources)
    arrived = lax.all_to_all(coefficients, "tile", split_axis=1, concat_axis=2, tiled=True)
    rows_local = arrived.shape[1]
    columns_all = arrived.shape[2]
    arrived = arrived.reshape(2, rows_local, columns_all, rank_positions, virtual_sources)
    receiver_factors = u_factors[0]
    real_arrived, imag_arrived = arrived[0], arrived[1]
    stacked_arrived = jnp.stack(
        [jnp.stack([real_arrived, -imag_arrived]), jnp.stack([imag_arrived, real_arrived])]
    )
    receivers = rows_local * tile_width
    received = (
        jnp.einsum(
            "imdlh,oimdlu->oumh",
            receiver_factors,
            stacked_arrived,
            preferred_element_type=jnp.float32,
        )
        .reshape(1, 2, virtual_sources, receivers)
        .astype(jnp.bfloat16)
    )
    piece = lax.all_gather(received, "freq", axis=0, tiled=True)
    count = piece.shape[0]

    backward = jnp.stack([cosine.T, -sine.T], 2).reshape(time_count, count * 2)
    added = jnp.dot(
        spread_over(backward, virtual_sources),
        piece.reshape(count * 2 * virtual_sources, receivers),
        preferred_element_type=jnp.float32,
    )
    scale_freq = 1.0 / math.sqrt(freq_total)
    return (added * scale_freq).astype(jnp.bfloat16).reshape(time_count, virtual_sources, receivers)


def solution(mesh):
    placed = (
        P("freq", "groups", "tile"),
        P("freq", None, None, "tile", None, None),
        P("freq", None, "tile", None, None, None),
        P("freq", None, "tile"),
    )
    return jax.shard_map(
        per_device,
        mesh=mesh,
        in_specs=placed,
        out_specs=P("freq", "groups", "tile"),
        check_vma=False,
    )
```

```python
import math

import jax
import jax.numpy as jnp
from jax import lax
from jax.sharding import PartitionSpec as P

NT = 640
F0 = 40


def twiddle(freq_ids, time_ids):
    turns = (F0 + freq_ids)[:, None] * time_ids[None, :] % NT
    angle = turns.astype(jnp.float32) * (2.0 * math.pi / NT)
    return (jnp.cos(angle).astype(jnp.bfloat16), jnp.sin(angle).astype(jnp.bfloat16))


def spread_over(weights, count):
    rows, cols = weights.shape
    kind = weights.dtype
    repeat_rows = (
        jnp.arange(rows * count, dtype=jnp.int32)[:, None] // count
        == jnp.arange(rows, dtype=jnp.int32)[None, :]
    ).astype(kind)
    repeat_cols = (
        jnp.arange(cols, dtype=jnp.int32)[:, None]
        == jnp.arange(cols * count, dtype=jnp.int32)[None, :] // count
    ).astype(kind)
    tall = jnp.dot(repeat_rows, weights, preferred_element_type=jnp.float32).astype(kind)
    wide = jnp.dot(tall, repeat_cols, preferred_element_type=jnp.float32)
    same = (
        jnp.arange(rows * count, dtype=jnp.int32)[:, None] % count
        == jnp.arange(cols * count, dtype=jnp.int32)[None, :] % count
    )
    return jnp.where(same, wide, jnp.float32(0.0)).astype(kind)


def per_device(traces, v_factors, u_factors, ranks):
    time_count = traces.shape[0]
    virtual_sources = traces.shape[1]
    source_count = traces.shape[2]
    freq_local = v_factors.shape[0]
    freq_total = freq_local * lax.axis_size("freq")
    tile_width = v_factors.shape[5]
    rank_positions = v_factors.shape[4]
    rows_all = v_factors.shape[2]
    columns = v_factors.shape[3]
    time_ids = lax.axis_index("freq") * time_count + jnp.arange(time_count, dtype=jnp.int32)
    scale_time = 1.0 / math.sqrt(NT)
    freq_ids = jnp.arange(freq_total, dtype=jnp.int32)
    cosine, sine = twiddle(freq_ids, time_ids)

    forward = jnp.stack([cosine, -sine], 1).reshape(freq_total * 2, time_count)
    flat_traces = traces.reshape(time_count * virtual_sources, source_count)
    partial = jnp.dot(
        spread_over(forward, virtual_sources), flat_traces, preferred_element_type=jnp.float32
    ).reshape(freq_total, 2, virtual_sources, source_count)
    gathered = lax.all_to_all(partial, "freq", split_axis=0, concat_axis=0, tiled=True)
    summed = gathered.reshape(
        lax.axis_size("freq"), freq_local, 2, virtual_sources, source_count
    ).sum(axis=0)
    spectrum = (summed * scale_time).astype(jnp.bfloat16)[0]
    spectral_tiles = spectrum.reshape(2, virtual_sources, columns, tile_width)
    emitter_factors = v_factors[0]
    real_part, imag_part = spectral_tiles[0], spectral_tiles[1]
    stacked_spectrum = jnp.stack(
        [jnp.stack([real_part, -imag_part]), jnp.stack([imag_part, real_part])]
    )
    stacked = jnp.einsum(
        "iajrs,oivjs->oajrv",
        emitter_factors,
        stacked_spectrum,
        preferred_element_type=jnp.float32,
    )
    rank_mask = (
        jnp.arange(rank_positions, dtype=jnp.int32)[None, None, :, None]
        < ranks[0][:, :, None, None]
    )
    coefficients = jnp.where(rank_mask[None], stacked, jnp.float32(0.0)).astype(jnp.bfloat16)
    coefficients = coefficients.reshape(2, rows_all, columns, rank_positions * virtual_sources)
    arrived = lax.all_to_all(coefficients, "tile", split_axis=1, concat_axis=2, tiled=True)
    rows_local = arrived.shape[1]
    columns_all = arrived.shape[2]
    arrived = arrived.reshape(2, rows_local, columns_all, rank_positions, virtual_sources)
    receiver_factors = u_factors[0]
    real_arrived, imag_arrived = arrived[0], arrived[1]
    stacked_arrived = jnp.stack(
        [jnp.stack([real_arrived, -imag_arrived]), jnp.stack([imag_arrived, real_arrived])]
    )
    receivers = rows_local * tile_width
    received = (
        jnp.einsum(
            "imdlh,oimdlu->oumh",
            receiver_factors,
            stacked_arrived,
            preferred_element_type=jnp.float32,
        )
        .reshape(1, 2, virtual_sources, receivers)
        .astype(jnp.bfloat16)
    )
    count = freq_total
    piece = lax.all_gather(received.reshape(-1), "freq", axis=0, tiled=True)

    backward = jnp.stack([cosine.T, -sine.T], 2).reshape(time_count, count * 2)
    added = jnp.dot(
        spread_over(backward, virtual_sources),
        piece.reshape(count * 2 * virtual_sources, receivers),
        preferred_element_type=jnp.float32,
    )
    scale_freq = 1.0 / math.sqrt(freq_total)
    return (added * scale_freq).astype(jnp.bfloat16).reshape(time_count, virtual_sources, receivers)


def solution(mesh):
    placed = (
        P("freq", "groups", "tile"),
        P("freq", None, None, "tile", None, None),
        P("freq", None, "tile", None, None, None),
        P("freq", None, "tile"),
    )
    return jax.shard_map(
        per_device,
        mesh=mesh,
        in_specs=placed,
        out_specs=P("freq", "groups", "tile"),
        check_vma=False,
    )
```

```python
import math

import jax
import jax.numpy as jnp
from jax import lax
from jax.sharding import PartitionSpec as P

NT = 640
F0 = 40


def twiddle(freq_ids, time_ids):
    turns = (F0 + freq_ids)[:, None] * time_ids[None, :] % NT
    angle = turns.astype(jnp.float32) * (2.0 * math.pi / NT)
    return (jnp.cos(angle).astype(jnp.bfloat16), jnp.sin(angle).astype(jnp.bfloat16))


def spread_over(weights, count):
    rows, cols = weights.shape
    kind = weights.dtype
    repeat_rows = (
        jnp.arange(rows * count, dtype=jnp.int32)[:, None] // count
        == jnp.arange(rows, dtype=jnp.int32)[None, :]
    ).astype(kind)
    repeat_cols = (
        jnp.arange(cols, dtype=jnp.int32)[:, None]
        == jnp.arange(cols * count, dtype=jnp.int32)[None, :] // count
    ).astype(kind)
    tall = jnp.dot(repeat_rows, weights, preferred_element_type=jnp.float32).astype(kind)
    wide = jnp.dot(tall, repeat_cols, preferred_element_type=jnp.float32)
    same = (
        jnp.arange(rows * count, dtype=jnp.int32)[:, None] % count
        == jnp.arange(cols * count, dtype=jnp.int32)[None, :] % count
    )
    return jnp.where(same, wide, jnp.float32(0.0)).astype(kind)


def per_device(traces, v_factors, u_factors, ranks):
    time_count = traces.shape[0]
    virtual_sources = traces.shape[1]
    source_count = traces.shape[2]
    freq_local = v_factors.shape[0]
    freq_total = freq_local * lax.axis_size("freq")
    tile_width = v_factors.shape[5]
    rank_positions = v_factors.shape[4]
    rows_all = v_factors.shape[2]
    columns = v_factors.shape[3]
    time_ids = lax.axis_index("freq") * time_count + jnp.arange(time_count, dtype=jnp.int32)
    scale_time = 1.0 / math.sqrt(NT)
    freq_ids = jnp.arange(freq_total, dtype=jnp.int32)
    cosine, sine = twiddle(freq_ids, time_ids)

    forward = jnp.stack([cosine, -sine], 1).reshape(freq_total * 2, time_count)
    flat_traces = traces.reshape(time_count * virtual_sources, source_count)
    partial = jnp.dot(
        spread_over(forward, virtual_sources), flat_traces, preferred_element_type=jnp.float32
    ).reshape(freq_total, 2, virtual_sources, source_count)
    gathered = lax.all_to_all(partial, "freq", split_axis=0, concat_axis=0, tiled=True)
    real_u, imag_u = u_factors[0, 0], u_factors[0, 1]
    receiver_factors = jnp.stack([jnp.stack([real_u, -imag_u]), jnp.stack([imag_u, real_u])])
    gathered, receiver_factors = lax.optimization_barrier((gathered, receiver_factors))
    summed = gathered.reshape(
        lax.axis_size("freq"), freq_local, 2, virtual_sources, source_count
    ).sum(axis=0)
    spectrum = (summed * scale_time).astype(jnp.bfloat16)[0]
    spectral_tiles = spectrum.reshape(2, virtual_sources, columns, tile_width)
    emitter_factors = v_factors[0]
    real_part, imag_part = spectral_tiles[0], spectral_tiles[1]
    stacked_spectrum = jnp.stack(
        [jnp.stack([real_part, -imag_part]), jnp.stack([imag_part, real_part])]
    )
    stacked = jnp.einsum(
        "iajrs,oivjs->oajrv",
        emitter_factors,
        stacked_spectrum,
        preferred_element_type=jnp.float32,
    )
    rank_mask = (
        jnp.arange(rank_positions, dtype=jnp.int32)[None, None, :, None]
        < ranks[0][:, :, None, None]
    )
    coefficients = jnp.where(rank_mask[None], stacked, jnp.float32(0.0)).astype(jnp.bfloat16)
    coefficients = coefficients.reshape(2, rows_all, columns, rank_positions * virtual_sources)
    arrived = lax.all_to_all(coefficients, "tile", split_axis=1, concat_axis=2, tiled=True)
    rows_local = arrived.shape[1]
    columns_all = arrived.shape[2]
    arrived = arrived.reshape(2, rows_local, columns_all, rank_positions, virtual_sources)
    receivers = rows_local * tile_width
    received = (
        jnp.einsum(
            "oimdlh,imdlu->oumh",
            receiver_factors,
            arrived,
            preferred_element_type=jnp.float32,
        )
        .reshape(1, 2, virtual_sources, receivers)
        .astype(jnp.bfloat16)
    )
    piece = lax.all_gather(received, "freq", axis=0, tiled=True)
    count = piece.shape[0]

    backward = jnp.stack([cosine.T, -sine.T], 2).reshape(time_count, count * 2)
    added = jnp.dot(
        spread_over(backward, virtual_sources),
        piece.reshape(count * 2 * virtual_sources, receivers),
        preferred_element_type=jnp.float32,
    )
    scale_freq = 1.0 / math.sqrt(freq_total)
    return (added * scale_freq).astype(jnp.bfloat16).reshape(time_count, virtual_sources, receivers)


def solution(mesh):
    placed = (
        P("freq", "groups", "tile"),
        P("freq", None, None, "tile", None, None),
        P("freq", None, "tile", None, None, None),
        P("freq", None, "tile"),
    )
    return jax.shard_map(
        per_device,
        mesh=mesh,
        in_specs=placed,
        out_specs=P("freq", "groups", "tile"),
        check_vma=False,
    )
```

```python
import math

import jax
import jax.numpy as jnp
from jax import lax
from jax.sharding import PartitionSpec as P

NT = 640
F0 = 40


def twiddle(freq_ids, time_ids):
    turns = (F0 + freq_ids)[:, None] * time_ids[None, :] % NT
    angle = turns.astype(jnp.float32) * (2.0 * math.pi / NT)
    return (jnp.cos(angle).astype(jnp.bfloat16), jnp.sin(angle).astype(jnp.bfloat16))


def spread_over(weights, count):
    rows, cols = weights.shape
    kind = weights.dtype
    repeat_rows = (
        jnp.arange(rows * count, dtype=jnp.int32)[:, None] // count
        == jnp.arange(rows, dtype=jnp.int32)[None, :]
    ).astype(kind)
    repeat_cols = (
        jnp.arange(cols, dtype=jnp.int32)[:, None]
        == jnp.arange(cols * count, dtype=jnp.int32)[None, :] // count
    ).astype(kind)
    tall = jnp.dot(repeat_rows, weights, preferred_element_type=jnp.float32).astype(kind)
    wide = jnp.dot(tall, repeat_cols, preferred_element_type=jnp.float32)
    same = (
        jnp.arange(rows * count, dtype=jnp.int32)[:, None] % count
        == jnp.arange(cols * count, dtype=jnp.int32)[None, :] % count
    )
    return jnp.where(same, wide, jnp.float32(0.0)).astype(kind)


def per_device(traces, v_factors, u_factors, ranks):
    time_count = traces.shape[0]
    virtual_sources = traces.shape[1]
    source_count = traces.shape[2]
    freq_local = v_factors.shape[0]
    freq_total = freq_local * lax.axis_size("freq")
    tile_width = v_factors.shape[5]
    rank_positions = v_factors.shape[4]
    rows_all = v_factors.shape[2]
    columns = v_factors.shape[3]
    time_ids = lax.axis_index("freq") * time_count + jnp.arange(time_count, dtype=jnp.int32)
    scale_time = 1.0 / math.sqrt(NT)
    freq_ids = jnp.arange(freq_total, dtype=jnp.int32)
    cosine, sine = twiddle(freq_ids, time_ids)

    forward = jnp.stack([cosine, -sine], 1).reshape(freq_total * 2, time_count)
    flat_traces = traces.reshape(time_count * virtual_sources, source_count)
    partial = jnp.dot(
        spread_over(forward, virtual_sources), flat_traces, preferred_element_type=jnp.float32
    ).reshape(freq_total, 2, virtual_sources, source_count)
    gathered = lax.all_to_all(
        partial.reshape(freq_total, -1), "freq", split_axis=0, concat_axis=0, tiled=True
    )
    summed = gathered.reshape(
        lax.axis_size("freq"), freq_local, 2, virtual_sources, source_count
    ).sum(axis=0)
    spectrum = (summed * scale_time).astype(jnp.bfloat16)[0]
    spectral_tiles = spectrum.reshape(2, virtual_sources, columns, tile_width)
    emitter_factors = v_factors[0]
    real_part, imag_part = spectral_tiles[0], spectral_tiles[1]
    stacked_spectrum = jnp.stack(
        [jnp.stack([real_part, -imag_part]), jnp.stack([imag_part, real_part])]
    )
    stacked = jnp.einsum(
        "iajrs,oivjs->oajrv",
        emitter_factors,
        stacked_spectrum,
        preferred_element_type=jnp.float32,
    )
    rank_mask = (
        jnp.arange(rank_positions, dtype=jnp.int32)[None, None, :, None]
        < ranks[0][:, :, None, None]
    )
    coefficients = jnp.where(rank_mask[None], stacked, jnp.float32(0.0)).astype(jnp.bfloat16)
    coefficients = coefficients.reshape(2, rows_all, columns, rank_positions * virtual_sources)
    arrived = lax.all_to_all(coefficients, "tile", split_axis=1, concat_axis=2, tiled=True)
    rows_local = arrived.shape[1]
    columns_all = arrived.shape[2]
    arrived = arrived.reshape(2, rows_local, columns_all, rank_positions, virtual_sources)
    receiver_factors = u_factors[0]
    real_arrived, imag_arrived = arrived[0], arrived[1]
    stacked_arrived = jnp.stack(
        [jnp.stack([real_arrived, -imag_arrived]), jnp.stack([imag_arrived, real_arrived])]
    )
    receivers = rows_local * tile_width
    received = (
        jnp.einsum(
            "imdlh,oimdlu->oumh",
            receiver_factors,
            stacked_arrived,
            preferred_element_type=jnp.float32,
        )
        .reshape(1, 2, virtual_sources, receivers)
        .astype(jnp.bfloat16)
    )
    piece = lax.all_gather(received, "freq", axis=0, tiled=True)
    count = piece.shape[0]

    backward = jnp.stack([cosine.T, -sine.T], 2).reshape(time_count, count * 2)
    added = jnp.dot(
        spread_over(backward, virtual_sources),
        piece.reshape(count * 2 * virtual_sources, receivers),
        preferred_element_type=jnp.float32,
    )
    scale_freq = 1.0 / math.sqrt(freq_total)
    return (added * scale_freq).astype(jnp.bfloat16).reshape(time_count, virtual_sources, receivers)


def solution(mesh):
    placed = (
        P("freq", "groups", "tile"),
        P("freq", None, None, "tile", None, None),
        P("freq", None, "tile", None, None, None),
        P("freq", None, "tile"),
    )
    return jax.shard_map(
        per_device,
        mesh=mesh,
        in_specs=placed,
        out_specs=P("freq", "groups", "tile"),
        check_vma=False,
    )
```

```python
import math

import jax
import jax.numpy as jnp
from jax import lax
from jax.sharding import PartitionSpec as P

NT = 640
F0 = 40


def twiddle(freq_ids, time_ids):
    turns = (F0 + freq_ids)[:, None] * time_ids[None, :] % NT
    angle = turns.astype(jnp.float32) * (2.0 * math.pi / NT)
    return (jnp.cos(angle).astype(jnp.bfloat16), jnp.sin(angle).astype(jnp.bfloat16))


def spread_over(weights, count):
    rows, cols = weights.shape
    kind = weights.dtype
    repeat_rows = (
        jnp.arange(rows * count, dtype=jnp.int32)[:, None] // count
        == jnp.arange(rows, dtype=jnp.int32)[None, :]
    ).astype(kind)
    repeat_cols = (
        jnp.arange(cols, dtype=jnp.int32)[:, None]
        == jnp.arange(cols * count, dtype=jnp.int32)[None, :] // count
    ).astype(kind)
    tall = jnp.dot(repeat_rows, weights, preferred_element_type=jnp.float32).astype(kind)
    wide = jnp.dot(tall, repeat_cols, preferred_element_type=jnp.float32)
    same = (
        jnp.arange(rows * count, dtype=jnp.int32)[:, None] % count
        == jnp.arange(cols * count, dtype=jnp.int32)[None, :] % count
    )
    return jnp.where(same, wide, jnp.float32(0.0)).astype(kind)


def per_device(traces, v_factors, u_factors, ranks):
    time_count = traces.shape[0]
    virtual_sources = traces.shape[1]
    source_count = traces.shape[2]
    freq_local = v_factors.shape[0]
    freq_total = freq_local * lax.axis_size("freq")
    tile_width = v_factors.shape[5]
    rank_positions = v_factors.shape[4]
    rows_all = v_factors.shape[2]
    columns = v_factors.shape[3]
    time_ids = lax.axis_index("freq") * time_count + jnp.arange(time_count, dtype=jnp.int32)
    scale_time = 1.0 / math.sqrt(NT)
    freq_ids = jnp.arange(freq_total, dtype=jnp.int32)
    cosine, sine = twiddle(freq_ids, time_ids)

    forward = jnp.stack([cosine, -sine], 1).reshape(freq_total * 2, time_count)
    flat_traces = traces.reshape(time_count * virtual_sources, source_count)
    partial = jnp.dot(
        spread_over(forward, virtual_sources), flat_traces, preferred_element_type=jnp.float32
    )
    gathered = lax.all_to_all(partial, "freq", split_axis=0, concat_axis=0, tiled=True)
    summed = gathered.reshape(
        lax.axis_size("freq"), freq_local, 2, virtual_sources, source_count
    ).sum(axis=0)
    spectrum = (summed * scale_time).astype(jnp.bfloat16)[0]
    spectral_tiles = spectrum.reshape(2, virtual_sources, columns, tile_width)
    emitter_factors = v_factors[0]
    real_part, imag_part = spectral_tiles[0], spectral_tiles[1]
    stacked_spectrum = jnp.stack(
        [jnp.stack([real_part, -imag_part]), jnp.stack([imag_part, real_part])]
    )
    stacked = jnp.einsum(
        "iajrs,oivjs->oajrv",
        emitter_factors,
        stacked_spectrum,
        preferred_element_type=jnp.float32,
    )
    rank_mask = (
        jnp.arange(rank_positions, dtype=jnp.int32)[None, None, :, None]
        < ranks[0][:, :, None, None]
    )
    coefficients = jnp.where(rank_mask[None], stacked, jnp.float32(0.0)).astype(jnp.bfloat16)
    coefficients = coefficients.reshape(2, rows_all, columns, rank_positions * virtual_sources)
    arrived = lax.all_to_all(coefficients, "tile", split_axis=1, concat_axis=2, tiled=True)
    rows_local = arrived.shape[1]
    columns_all = arrived.shape[2]
    arrived = arrived.reshape(2, rows_local, columns_all, rank_positions, virtual_sources)
    receiver_factors = u_factors[0]
    real_arrived, imag_arrived = arrived[0], arrived[1]
    stacked_arrived = jnp.stack(
        [jnp.stack([real_arrived, -imag_arrived]), jnp.stack([imag_arrived, real_arrived])]
    )
    receivers = rows_local * tile_width
    received = (
        jnp.einsum(
            "imdlh,oimdlu->oumh",
            receiver_factors,
            stacked_arrived,
            preferred_element_type=jnp.float32,
        )
        .reshape(1, 2, virtual_sources, receivers)
        .astype(jnp.bfloat16)
    )
    piece = lax.all_gather(received, "freq", axis=0, tiled=True)
    count = piece.shape[0]

    backward = jnp.stack([cosine.T, -sine.T], 2).reshape(time_count, count * 2)
    added = jnp.dot(
        spread_over(backward, virtual_sources),
        piece.reshape(count * 2 * virtual_sources, receivers),
        preferred_element_type=jnp.float32,
    )
    scale_freq = 1.0 / math.sqrt(freq_total)
    return (added * scale_freq).astype(jnp.bfloat16).reshape(time_count, virtual_sources, receivers)


def solution(mesh):
    placed = (
        P("freq", "groups", "tile"),
        P("freq", None, None, "tile", None, None),
        P("freq", None, "tile", None, None, None),
        P("freq", None, "tile"),
    )
    return jax.shard_map(
        per_device,
        mesh=mesh,
        in_specs=placed,
        out_specs=P("freq", "groups", "tile"),
        check_vma=False,
    )
```

```python
import math

import jax
import jax.numpy as jnp
from jax import lax
from jax.sharding import PartitionSpec as P

NT = 640
F0 = 40


def twiddle(freq_ids, time_ids):
    turns = (F0 + freq_ids)[:, None] * time_ids[None, :] % NT
    angle = turns.astype(jnp.float32) * (2.0 * math.pi / NT)
    return (jnp.cos(angle).astype(jnp.bfloat16), jnp.sin(angle).astype(jnp.bfloat16))


def spread_over(weights, count):
    rows, cols = weights.shape
    kind = weights.dtype
    repeat_rows = (
        jnp.arange(rows * count, dtype=jnp.int32)[:, None] // count
        == jnp.arange(rows, dtype=jnp.int32)[None, :]
    ).astype(kind)
    repeat_cols = (
        jnp.arange(cols, dtype=jnp.int32)[:, None]
        == jnp.arange(cols * count, dtype=jnp.int32)[None, :] // count
    ).astype(kind)
    tall = jnp.dot(repeat_rows, weights, preferred_element_type=jnp.float32).astype(kind)
    wide = jnp.dot(tall, repeat_cols, preferred_element_type=jnp.float32)
    same = (
        jnp.arange(rows * count, dtype=jnp.int32)[:, None] % count
        == jnp.arange(cols * count, dtype=jnp.int32)[None, :] % count
    )
    return jnp.where(same, wide, jnp.float32(0.0)).astype(kind)


def per_device(traces, v_factors, u_factors, ranks):
    time_count = traces.shape[0]
    virtual_sources = traces.shape[1]
    source_count = traces.shape[2]
    freq_local = v_factors.shape[0]
    freq_total = freq_local * lax.axis_size("freq")
    tile_width = v_factors.shape[5]
    rank_positions = v_factors.shape[4]
    rows_all = v_factors.shape[2]
    columns = v_factors.shape[3]
    time_ids = lax.axis_index("freq") * time_count + jnp.arange(time_count, dtype=jnp.int32)
    scale_time = 1.0 / math.sqrt(NT)
    freq_ids = jnp.arange(freq_total, dtype=jnp.int32)
    cosine, sine = twiddle(freq_ids, time_ids)

    forward = jnp.stack([cosine, -sine], 1).reshape(freq_total * 2, time_count)
    flat_traces = traces.reshape(time_count * virtual_sources, source_count)
    weights = spread_over(forward, virtual_sources)
    halves = 2 if source_count % 256 == 0 else 1
    span = source_count // halves
    partial = jnp.concatenate(
        [
            jnp.dot(
                weights,
                flat_traces[:, half * span:(half + 1) * span],
                preferred_element_type=jnp.float32,
            )
            for half in range(halves)
        ],
        axis=1,
    )
    gathered = lax.all_to_all(partial, "freq", split_axis=0, concat_axis=0, tiled=True)
    summed = gathered.reshape(
        lax.axis_size("freq"), freq_local, 2, virtual_sources, source_count
    ).sum(axis=0)
    spectrum = (summed * scale_time).astype(jnp.bfloat16)[0]
    spectral_tiles = spectrum.reshape(2, virtual_sources, columns, tile_width)
    emitter_factors = v_factors[0]
    real_part, imag_part = spectral_tiles[0], spectral_tiles[1]
    stacked_spectrum = jnp.stack(
        [jnp.stack([real_part, -imag_part]), jnp.stack([imag_part, real_part])]
    )
    stacked = jnp.einsum(
        "iajrs,oivjs->oajrv",
        emitter_factors,
        stacked_spectrum,
        preferred_element_type=jnp.float32,
    )
    rank_mask = (
        jnp.arange(rank_positions, dtype=jnp.int32)[None, None, :, None]
        < ranks[0][:, :, None, None]
    )
    coefficients = jnp.where(rank_mask[None], stacked, jnp.float32(0.0)).astype(jnp.bfloat16)
    coefficients = coefficients.reshape(2, rows_all, columns, rank_positions * virtual_sources)
    arrived = lax.all_to_all(coefficients, "tile", split_axis=1, concat_axis=2, tiled=True)
    rows_local = arrived.shape[1]
    columns_all = arrived.shape[2]
    arrived = arrived.reshape(2, rows_local, columns_all, rank_positions, virtual_sources)
    receiver_factors = u_factors[0]
    real_arrived, imag_arrived = arrived[0], arrived[1]
    stacked_arrived = jnp.stack(
        [jnp.stack([real_arrived, -imag_arrived]), jnp.stack([imag_arrived, real_arrived])]
    )
    receivers = rows_local * tile_width
    received = (
        jnp.einsum(
            "imdlh,oimdlu->oumh",
            receiver_factors,
            stacked_arrived,
            preferred_element_type=jnp.float32,
        )
        .reshape(1, 2, virtual_sources, receivers)
        .astype(jnp.bfloat16)
    )
    piece = lax.all_gather(received, "freq", axis=0, tiled=True)
    count = piece.shape[0]

    backward = jnp.stack([cosine.T, -sine.T], 2).reshape(time_count, count * 2)
    added = jnp.dot(
        spread_over(backward, virtual_sources),
        piece.reshape(count * 2 * virtual_sources, receivers),
        preferred_element_type=jnp.float32,
    )
    scale_freq = 1.0 / math.sqrt(freq_total)
    return (added * scale_freq).astype(jnp.bfloat16).reshape(time_count, virtual_sources, receivers)


def solution(mesh):
    placed = (
        P("freq", "groups", "tile"),
        P("freq", None, None, "tile", None, None),
        P("freq", None, "tile", None, None, None),
        P("freq", None, "tile"),
    )
    return jax.shard_map(
        per_device,
        mesh=mesh,
        in_specs=placed,
        out_specs=P("freq", "groups", "tile"),
        check_vma=False,
    )
```

```python
import math

import jax
import jax.numpy as jnp
from jax import lax
from jax.sharding import PartitionSpec as P

NT = 640
F0 = 40


def twiddle(freq_ids, time_ids):
    turns = (F0 + freq_ids)[:, None] * time_ids[None, :] % NT
    angle = turns.astype(jnp.float32) * (2.0 * math.pi / NT)
    return (jnp.cos(angle).astype(jnp.bfloat16), jnp.sin(angle).astype(jnp.bfloat16))


def spread_over(weights, count):
    rows, cols = weights.shape
    kind = weights.dtype
    repeat_rows = (
        jnp.arange(rows * count, dtype=jnp.int32)[:, None] // count
        == jnp.arange(rows, dtype=jnp.int32)[None, :]
    ).astype(kind)
    repeat_cols = (
        jnp.arange(cols, dtype=jnp.int32)[:, None]
        == jnp.arange(cols * count, dtype=jnp.int32)[None, :] // count
    ).astype(kind)
    tall = jnp.dot(repeat_rows, weights, preferred_element_type=jnp.float32).astype(kind)
    wide = jnp.dot(tall, repeat_cols, preferred_element_type=jnp.float32)
    same = (
        jnp.arange(rows * count, dtype=jnp.int32)[:, None] % count
        == jnp.arange(cols * count, dtype=jnp.int32)[None, :] % count
    )
    return jnp.where(same, wide, jnp.float32(0.0)).astype(kind)


def line_reduce_scatter(partial, axis):
    count = partial.shape[0]
    own = lax.axis_index(axis)

    def block(index):
        return lax.dynamic_index_in_dim(partial, jnp.clip(index, 0, count - 1), 0, keepdims=False)

    right = jnp.zeros_like(partial[0])
    left = jnp.zeros_like(partial[0])
    for step in range(1, count):
        send_right = block(count - step + own) + right
        send_left = block(own + step - count) + left
        right = lax.ppermute(send_right, axis, [(p, p + 1) for p in range(step)])
        left = lax.ppermute(send_left, axis, [(count - 1 - p, count - 2 - p) for p in range(step)])
    return block(own) + right + left


def per_device(traces, v_factors, u_factors, ranks):
    time_count = traces.shape[0]
    virtual_sources = traces.shape[1]
    source_count = traces.shape[2]
    freq_local = v_factors.shape[0]
    freq_total = freq_local * lax.axis_size("freq")
    tile_width = v_factors.shape[5]
    rank_positions = v_factors.shape[4]
    rows_all = v_factors.shape[2]
    columns = v_factors.shape[3]
    time_ids = lax.axis_index("freq") * time_count + jnp.arange(time_count, dtype=jnp.int32)
    scale_time = 1.0 / math.sqrt(NT)
    freq_ids = jnp.arange(freq_total, dtype=jnp.int32)
    cosine, sine = twiddle(freq_ids, time_ids)

    forward = jnp.stack([cosine, -sine], 1).reshape(freq_total * 2, time_count)
    flat_traces = traces.reshape(time_count * virtual_sources, source_count)
    partial = jnp.dot(
        spread_over(forward, virtual_sources), flat_traces, preferred_element_type=jnp.float32
    ).reshape(freq_total, 2, virtual_sources, source_count)
    gathered = lax.all_to_all(partial[:, 0], "freq", split_axis=0, concat_axis=0, tiled=True)
    real_sum = gathered.reshape(
        lax.axis_size("freq"), freq_local, virtual_sources, source_count
    ).sum(axis=0)
    imag_sum = line_reduce_scatter(partial[:, 1], "freq")[None]
    summed = jnp.stack([real_sum, imag_sum], axis=1)
    spectrum = (summed * scale_time).astype(jnp.bfloat16)[0]
    spectral_tiles = spectrum.reshape(2, virtual_sources, columns, tile_width)
    emitter_factors = v_factors[0]
    real_part, imag_part = spectral_tiles[0], spectral_tiles[1]
    stacked_spectrum = jnp.stack(
        [jnp.stack([real_part, -imag_part]), jnp.stack([imag_part, real_part])]
    )
    stacked = jnp.einsum(
        "iajrs,oivjs->oajrv",
        emitter_factors,
        stacked_spectrum,
        preferred_element_type=jnp.float32,
    )
    rank_mask = (
        jnp.arange(rank_positions, dtype=jnp.int32)[None, None, :, None]
        < ranks[0][:, :, None, None]
    )
    coefficients = jnp.where(rank_mask[None], stacked, jnp.float32(0.0)).astype(jnp.bfloat16)
    coefficients = coefficients.reshape(2, rows_all, columns, rank_positions * virtual_sources)
    arrived = lax.all_to_all(coefficients, "tile", split_axis=1, concat_axis=2, tiled=True)
    rows_local = arrived.shape[1]
    columns_all = arrived.shape[2]
    arrived = arrived.reshape(2, rows_local, columns_all, rank_positions, virtual_sources)
    receiver_factors = u_factors[0]
    real_arrived, imag_arrived = arrived[0], arrived[1]
    stacked_arrived = jnp.stack(
        [jnp.stack([real_arrived, -imag_arrived]), jnp.stack([imag_arrived, real_arrived])]
    )
    receivers = rows_local * tile_width
    received = (
        jnp.einsum(
            "imdlh,oimdlu->oumh",
            receiver_factors,
            stacked_arrived,
            preferred_element_type=jnp.float32,
        )
        .reshape(1, 2, virtual_sources, receivers)
        .astype(jnp.bfloat16)
    )
    piece = lax.all_gather(received, "freq", axis=0, tiled=True)
    count = piece.shape[0]

    backward = jnp.stack([cosine.T, -sine.T], 2).reshape(time_count, count * 2)
    added = jnp.dot(
        spread_over(backward, virtual_sources),
        piece.reshape(count * 2 * virtual_sources, receivers),
        preferred_element_type=jnp.float32,
    )
    scale_freq = 1.0 / math.sqrt(freq_total)
    return (added * scale_freq).astype(jnp.bfloat16).reshape(time_count, virtual_sources, receivers)


def solution(mesh):
    placed = (
        P("freq", "groups", "tile"),
        P("freq", None, None, "tile", None, None),
        P("freq", None, "tile", None, None, None),
        P("freq", None, "tile"),
    )
    return jax.shard_map(
        per_device,
        mesh=mesh,
        in_specs=placed,
        out_specs=P("freq", "groups", "tile"),
        check_vma=False,
    )
```

```python
import math

import jax
import jax.numpy as jnp
from jax import lax
from jax.sharding import PartitionSpec as P

NT = 640
F0 = 40


def twiddle(freq_ids, time_ids):
    turns = (F0 + freq_ids)[:, None] * time_ids[None, :] % NT
    angle = turns.astype(jnp.float32) * (2.0 * math.pi / NT)
    return (jnp.cos(angle).astype(jnp.bfloat16), jnp.sin(angle).astype(jnp.bfloat16))


def spread_over(weights, count):
    rows, cols = weights.shape
    kind = weights.dtype
    repeat_rows = (
        jnp.arange(rows * count, dtype=jnp.int32)[:, None] // count
        == jnp.arange(rows, dtype=jnp.int32)[None, :]
    ).astype(kind)
    repeat_cols = (
        jnp.arange(cols, dtype=jnp.int32)[:, None]
        == jnp.arange(cols * count, dtype=jnp.int32)[None, :] // count
    ).astype(kind)
    tall = jnp.dot(repeat_rows, weights, preferred_element_type=jnp.float32).astype(kind)
    wide = jnp.dot(tall, repeat_cols, preferred_element_type=jnp.float32)
    same = (
        jnp.arange(rows * count, dtype=jnp.int32)[:, None] % count
        == jnp.arange(cols * count, dtype=jnp.int32)[None, :] % count
    )
    return jnp.where(same, wide, jnp.float32(0.0)).astype(kind)


def per_device(traces, v_factors, u_factors, ranks):
    time_count = traces.shape[0]
    virtual_sources = traces.shape[1]
    source_count = traces.shape[2]
    freq_local = v_factors.shape[0]
    freq_total = freq_local * lax.axis_size("freq")
    tile_width = v_factors.shape[5]
    rank_positions = v_factors.shape[4]
    rows_all = v_factors.shape[2]
    columns = v_factors.shape[3]
    time_ids = lax.axis_index("freq") * time_count + jnp.arange(time_count, dtype=jnp.int32)
    scale_time = 1.0 / math.sqrt(NT)
    freq_ids = jnp.arange(freq_total, dtype=jnp.int32)
    cosine, sine = twiddle(freq_ids, time_ids)

    forward = jnp.stack([cosine, -sine], 1).reshape(freq_total * 2, time_count)
    flat_traces = traces.reshape(time_count * virtual_sources, source_count)
    partial = jnp.dot(
        spread_over(forward, virtual_sources), flat_traces, preferred_element_type=jnp.float32
    ).reshape(freq_total, 2, virtual_sources, source_count)
    gathered = lax.all_to_all(partial[:, ::-1], "freq", split_axis=0, concat_axis=0, tiled=True)
    summed = gathered.reshape(
        lax.axis_size("freq"), freq_local, 2, virtual_sources, source_count
    ).sum(axis=0)[:, ::-1]
    spectrum = (summed * scale_time).astype(jnp.bfloat16)[0]
    spectral_tiles = spectrum.reshape(2, virtual_sources, columns, tile_width)
    emitter_factors = v_factors[0]
    real_part, imag_part = spectral_tiles[0], spectral_tiles[1]
    stacked_spectrum = jnp.stack(
        [jnp.stack([real_part, -imag_part]), jnp.stack([imag_part, real_part])]
    )
    stacked = jnp.einsum(
        "iajrs,oivjs->oajrv",
        emitter_factors,
        stacked_spectrum,
        preferred_element_type=jnp.float32,
    )
    rank_mask = (
        jnp.arange(rank_positions, dtype=jnp.int32)[None, None, :, None]
        < ranks[0][:, :, None, None]
    )
    coefficients = jnp.where(rank_mask[None], stacked, jnp.float32(0.0)).astype(jnp.bfloat16)
    coefficients = coefficients.reshape(2, rows_all, columns, rank_positions * virtual_sources)
    arrived = lax.all_to_all(coefficients, "tile", split_axis=1, concat_axis=2, tiled=True)
    rows_local = arrived.shape[1]
    columns_all = arrived.shape[2]
    arrived = arrived.reshape(2, rows_local, columns_all, rank_positions, virtual_sources)
    receiver_factors = u_factors[0]
    real_arrived, imag_arrived = arrived[0], arrived[1]
    stacked_arrived = jnp.stack(
        [jnp.stack([real_arrived, -imag_arrived]), jnp.stack([imag_arrived, real_arrived])]
    )
    receivers = rows_local * tile_width
    received = (
        jnp.einsum(
            "imdlh,oimdlu->oumh",
            receiver_factors,
            stacked_arrived,
            preferred_element_type=jnp.float32,
        )
        .reshape(1, 2, virtual_sources, receivers)
        .astype(jnp.bfloat16)
    )
    piece = lax.all_gather(received, "freq", axis=0, tiled=True)
    count = piece.shape[0]

    backward = jnp.stack([cosine.T, -sine.T], 2).reshape(time_count, count * 2)
    added = jnp.dot(
        spread_over(backward, virtual_sources),
        piece.reshape(count * 2 * virtual_sources, receivers),
        preferred_element_type=jnp.float32,
    )
    scale_freq = 1.0 / math.sqrt(freq_total)
    return (added * scale_freq).astype(jnp.bfloat16).reshape(time_count, virtual_sources, receivers)


def solution(mesh):
    placed = (
        P("freq", "groups", "tile"),
        P("freq", None, None, "tile", None, None),
        P("freq", None, "tile", None, None, None),
        P("freq", None, "tile"),
    )
    return jax.shard_map(
        per_device,
        mesh=mesh,
        in_specs=placed,
        out_specs=P("freq", "groups", "tile"),
        check_vma=False,
    )
```

```python
import math

import jax
import jax.numpy as jnp
from jax import lax
from jax.sharding import PartitionSpec as P

NT = 640
F0 = 40


def twiddle(freq_ids, time_ids):
    turns = (F0 + freq_ids)[:, None] * time_ids[None, :] % NT
    angle = turns.astype(jnp.float32) * (2.0 * math.pi / NT)
    return (jnp.cos(angle).astype(jnp.bfloat16), jnp.sin(angle).astype(jnp.bfloat16))


def spread_over(weights, count):
    rows, cols = weights.shape
    kind = weights.dtype
    repeat_rows = (
        jnp.arange(rows * count, dtype=jnp.int32)[:, None] // count
        == jnp.arange(rows, dtype=jnp.int32)[None, :]
    ).astype(kind)
    repeat_cols = (
        jnp.arange(cols, dtype=jnp.int32)[:, None]
        == jnp.arange(cols * count, dtype=jnp.int32)[None, :] // count
    ).astype(kind)
    tall = jnp.dot(repeat_rows, weights, preferred_element_type=jnp.float32).astype(kind)
    wide = jnp.dot(tall, repeat_cols, preferred_element_type=jnp.float32)
    same = (
        jnp.arange(rows * count, dtype=jnp.int32)[:, None] % count
        == jnp.arange(cols * count, dtype=jnp.int32)[None, :] % count
    )
    return jnp.where(same, wide, jnp.float32(0.0)).astype(kind)


def per_device(traces, v_factors, u_factors, ranks):
    time_count = traces.shape[0]
    virtual_sources = traces.shape[1]
    source_count = traces.shape[2]
    freq_local = v_factors.shape[0]
    freq_total = freq_local * lax.axis_size("freq")
    tile_width = v_factors.shape[5]
    rank_positions = v_factors.shape[4]
    rows_all = v_factors.shape[2]
    columns = v_factors.shape[3]
    time_ids = lax.axis_index("freq") * time_count + jnp.arange(time_count, dtype=jnp.int32)
    scale_time = 1.0 / math.sqrt(NT)
    freq_ids = jnp.arange(freq_total, dtype=jnp.int32)
    cosine, sine = twiddle(freq_ids, time_ids)

    forward = jnp.stack([cosine, -sine], 1).reshape(freq_total * 2, time_count)
    flat_traces = traces.reshape(time_count * virtual_sources, source_count)
    partial = jnp.dot(
        spread_over(forward, virtual_sources), flat_traces, preferred_element_type=jnp.float32
    ).reshape(freq_total, 2, virtual_sources, source_count)
    gathered = lax.all_to_all(partial[:, ::-1], "freq", split_axis=0, concat_axis=0, tiled=True)
    real_u, imag_u = u_factors[0, 0], u_factors[0, 1]
    receiver_factors = jnp.stack([jnp.stack([real_u, -imag_u]), jnp.stack([imag_u, real_u])])
    gathered, receiver_factors = lax.optimization_barrier((gathered, receiver_factors))
    summed = gathered.reshape(
        lax.axis_size("freq"), freq_local, 2, virtual_sources, source_count
    ).sum(axis=0)[:, ::-1]
    spectrum = (summed * scale_time).astype(jnp.bfloat16)[0]
    spectral_tiles = spectrum.reshape(2, virtual_sources, columns, tile_width)
    emitter_factors = v_factors[0]
    real_part, imag_part = spectral_tiles[0], spectral_tiles[1]
    stacked_spectrum = jnp.stack(
        [jnp.stack([real_part, -imag_part]), jnp.stack([imag_part, real_part])]
    )
    stacked = jnp.einsum(
        "iajrs,oivjs->oajrv",
        emitter_factors,
        stacked_spectrum,
        preferred_element_type=jnp.float32,
    )
    rank_mask = (
        jnp.arange(rank_positions, dtype=jnp.int32)[None, None, :, None]
        < ranks[0][:, :, None, None]
    )
    coefficients = jnp.where(rank_mask[None], stacked, jnp.float32(0.0)).astype(jnp.bfloat16)
    coefficients = coefficients.reshape(2, rows_all, columns, rank_positions * virtual_sources)
    arrived = lax.all_to_all(coefficients, "tile", split_axis=1, concat_axis=2, tiled=True)
    rows_local = arrived.shape[1]
    columns_all = arrived.shape[2]
    arrived = arrived.reshape(2, rows_local, columns_all, rank_positions, virtual_sources)
    receivers = rows_local * tile_width
    received = (
        jnp.einsum(
            "oimdlh,imdlu->oumh",
            receiver_factors,
            arrived,
            preferred_element_type=jnp.float32,
        )
        .reshape(1, 2, virtual_sources, receivers)
        .astype(jnp.bfloat16)
    )
    piece = lax.all_gather(received, "freq", axis=0, tiled=True)
    count = piece.shape[0]

    backward = jnp.stack([cosine.T, -sine.T], 2).reshape(time_count, count * 2)
    added = jnp.dot(
        spread_over(backward, virtual_sources),
        piece.reshape(count * 2 * virtual_sources, receivers),
        preferred_element_type=jnp.float32,
    )
    scale_freq = 1.0 / math.sqrt(freq_total)
    return (added * scale_freq).astype(jnp.bfloat16).reshape(time_count, virtual_sources, receivers)


def solution(mesh):
    placed = (
        P("freq", "groups", "tile"),
        P("freq", None, None, "tile", None, None),
        P("freq", None, "tile", None, None, None),
        P("freq", None, "tile"),
    )
    return jax.shard_map(
        per_device,
        mesh=mesh,
        in_specs=placed,
        out_specs=P("freq", "groups", "tile"),
        check_vma=False,
    )
```

```python
import math

import jax
import jax.numpy as jnp
from jax import lax
from jax.sharding import PartitionSpec as P

NT = 640
F0 = 40


def twiddle(freq_ids, time_ids):
    turns = (F0 + freq_ids)[:, None] * time_ids[None, :] % NT
    angle = turns.astype(jnp.float32) * (2.0 * math.pi / NT)
    return (jnp.cos(angle).astype(jnp.bfloat16), jnp.sin(angle).astype(jnp.bfloat16))


def spread_over(weights, count):
    rows, cols = weights.shape
    kind = weights.dtype
    repeat_rows = (
        jnp.arange(rows * count, dtype=jnp.int32)[:, None] // count
        == jnp.arange(rows, dtype=jnp.int32)[None, :]
    ).astype(kind)
    repeat_cols = (
        jnp.arange(cols, dtype=jnp.int32)[:, None]
        == jnp.arange(cols * count, dtype=jnp.int32)[None, :] // count
    ).astype(kind)
    tall = jnp.dot(repeat_rows, weights, preferred_element_type=jnp.float32).astype(kind)
    wide = jnp.dot(tall, repeat_cols, preferred_element_type=jnp.float32)
    same = (
        jnp.arange(rows * count, dtype=jnp.int32)[:, None] % count
        == jnp.arange(cols * count, dtype=jnp.int32)[None, :] % count
    )
    return jnp.where(same, wide, jnp.float32(0.0)).astype(kind)


def per_device(traces, v_factors, u_factors, ranks):
    time_count = traces.shape[0]
    virtual_sources = traces.shape[1]
    source_count = traces.shape[2]
    freq_local = v_factors.shape[0]
    freq_total = freq_local * lax.axis_size("freq")
    tile_width = v_factors.shape[5]
    rank_positions = v_factors.shape[4]
    rows_all = v_factors.shape[2]
    columns = v_factors.shape[3]
    time_ids = lax.axis_index("freq") * time_count + jnp.arange(time_count, dtype=jnp.int32)
    scale_time = 1.0 / math.sqrt(NT)
    freq_ids = jnp.arange(freq_total, dtype=jnp.int32)
    cosine, sine = twiddle(freq_ids, time_ids)

    forward = jnp.stack([cosine, -sine], 1).reshape(freq_total * 2, time_count)
    flat_traces = traces.reshape(time_count * virtual_sources, source_count)
    partial = jnp.dot(
        spread_over(forward, virtual_sources), flat_traces, preferred_element_type=jnp.float32
    ).reshape(freq_total, 2, virtual_sources, source_count)
    gathered = lax.all_to_all(partial[:, ::-1], "freq", split_axis=0, concat_axis=0, tiled=True)
    summed = gathered.reshape(
        lax.axis_size("freq"), freq_local, 2, virtual_sources, source_count
    ).sum(axis=0)[:, ::-1]
    spectrum = (summed * scale_time).astype(jnp.bfloat16)[0]
    spectral_tiles = spectrum.reshape(2, virtual_sources, columns, tile_width)
    emitter_factors = v_factors[0]
    real_part, imag_part = spectral_tiles[0], spectral_tiles[1]
    stacked_spectrum = jnp.stack(
        [jnp.stack([real_part, -imag_part]), jnp.stack([imag_part, real_part])]
    )
    stacked = jnp.einsum(
        "iajrs,oivjs->oajrv",
        emitter_factors,
        stacked_spectrum,
        preferred_element_type=jnp.float32,
    )
    rank_mask = (
        jnp.arange(rank_positions, dtype=jnp.int32)[None, None, :, None]
        < ranks[0][:, :, None, None]
    )
    coefficients = jnp.where(rank_mask[None], stacked, jnp.float32(0.0)).astype(jnp.bfloat16)
    coefficients = coefficients.reshape(2, rows_all, columns, rank_positions * virtual_sources)
    arrived = lax.all_to_all(coefficients, "tile", split_axis=1, concat_axis=2, tiled=True)
    rows_local = arrived.shape[1]
    columns_all = arrived.shape[2]
    arrived = arrived.reshape(2, rows_local, columns_all, rank_positions, virtual_sources)
    receiver_factors = u_factors[0]
    real_arrived, imag_arrived = arrived[0], arrived[1]
    stacked_arrived = jnp.stack(
        [jnp.stack([real_arrived, -imag_arrived]), jnp.stack([imag_arrived, real_arrived])]
    )
    receivers = rows_local * tile_width
    received = (
        jnp.einsum(
            "imdlh,oimdlu->oumh",
            receiver_factors,
            stacked_arrived,
            preferred_element_type=jnp.float32,
        )
        .reshape(1, 2, virtual_sources, receivers)
        .astype(jnp.bfloat16)
    )
    piece = lax.all_gather(received, "freq", axis=0, tiled=True)
    count = piece.shape[0]

    backward = jnp.stack([cosine.T, -sine.T], 2).reshape(time_count, count * 2)
    scale_freq = 1.0 / math.sqrt(freq_total)
    exact_scale = math.log2(scale_freq).is_integer()
    if exact_scale:
        backward = backward * jnp.bfloat16(scale_freq)
    added = jnp.dot(
        spread_over(backward, virtual_sources),
        piece.reshape(count * 2 * virtual_sources, receivers),
        preferred_element_type=jnp.float32,
    )
    if not exact_scale:
        added = added * scale_freq
    return added.astype(jnp.bfloat16).reshape(time_count, virtual_sources, receivers)


def solution(mesh):
    placed = (
        P("freq", "groups", "tile"),
        P("freq", None, None, "tile", None, None),
        P("freq", None, "tile", None, None, None),
        P("freq", None, "tile"),
    )
    return jax.shard_map(
        per_device,
        mesh=mesh,
        in_specs=placed,
        out_specs=P("freq", "groups", "tile"),
        check_vma=False,
    )
```

```python
import math

import jax
import jax.numpy as jnp
from jax import lax
from jax.sharding import PartitionSpec as P

NT = 640
F0 = 40


def twiddle(freq_ids, time_ids):
    turns = (F0 + freq_ids)[:, None] * time_ids[None, :] % NT
    angle = turns.astype(jnp.float32) * (2.0 * math.pi / NT)
    return (jnp.cos(angle).astype(jnp.bfloat16), jnp.sin(angle).astype(jnp.bfloat16))


def spread_over(weights, count):
    rows, cols = weights.shape
    kind = weights.dtype
    repeat_rows = (
        jnp.arange(rows * count, dtype=jnp.int32)[:, None] // count
        == jnp.arange(rows, dtype=jnp.int32)[None, :]
    ).astype(kind)
    repeat_cols = (
        jnp.arange(cols, dtype=jnp.int32)[:, None]
        == jnp.arange(cols * count, dtype=jnp.int32)[None, :] // count
    ).astype(kind)
    tall = jnp.dot(repeat_rows, weights, preferred_element_type=jnp.float32).astype(kind)
    wide = jnp.dot(tall, repeat_cols, preferred_element_type=jnp.float32)
    same = (
        jnp.arange(rows * count, dtype=jnp.int32)[:, None] % count
        == jnp.arange(cols * count, dtype=jnp.int32)[None, :] % count
    )
    return jnp.where(same, wide, jnp.float32(0.0)).astype(kind)


def per_device(traces, v_factors, u_factors, ranks):
    time_count = traces.shape[0]
    virtual_sources = traces.shape[1]
    source_count = traces.shape[2]
    freq_local = v_factors.shape[0]
    freq_total = freq_local * lax.axis_size("freq")
    tile_width = v_factors.shape[5]
    rank_positions = v_factors.shape[4]
    rows_all = v_factors.shape[2]
    columns = v_factors.shape[3]
    time_ids = lax.axis_index("freq") * time_count + jnp.arange(time_count, dtype=jnp.int32)
    scale_time = 1.0 / math.sqrt(NT)
    freq_ids = jnp.arange(freq_total, dtype=jnp.int32)
    cosine, sine = twiddle(freq_ids, time_ids)

    forward = jnp.stack([cosine, -sine], 1).reshape(freq_total * 2, time_count)
    flat_traces = traces.reshape(time_count * virtual_sources, source_count)
    partial = jnp.dot(
        spread_over(forward, virtual_sources), flat_traces, preferred_element_type=jnp.float32
    ).reshape(freq_total, 2, virtual_sources, source_count)
    gathered = lax.all_to_all(partial[:, ::-1], "freq", split_axis=0, concat_axis=0, tiled=True)
    summed = gathered.reshape(
        lax.axis_size("freq"), freq_local, 2, virtual_sources, source_count
    ).sum(axis=0)[:, ::-1]
    spectrum = (summed * scale_time).astype(jnp.bfloat16)[0]
    spectral_tiles = spectrum.reshape(2, virtual_sources, columns, tile_width)
    emitter_factors = v_factors[0]
    real_part, imag_part = spectral_tiles[0], spectral_tiles[1]
    stacked_spectrum = jnp.stack(
        [jnp.stack([real_part, -imag_part]), jnp.stack([imag_part, real_part])]
    )
    stacked = jnp.einsum(
        "iajrs,oivjs->oajrv",
        emitter_factors,
        stacked_spectrum,
        preferred_element_type=jnp.float32,
    )
    rank_mask = (
        jnp.arange(rank_positions, dtype=jnp.int32)[None, None, :, None]
        < ranks[0][:, :, None, None]
    )
    coefficients = jnp.where(rank_mask[None], stacked, jnp.float32(0.0)).astype(jnp.bfloat16)
    tile_count = lax.axis_size("tile")
    rows_local = rows_all // tile_count
    columns_all = tile_count * columns
    coefficients = coefficients.reshape(
        2, tile_count, rows_local, columns, rank_positions * virtual_sources
    ).transpose(1, 0, 2, 3, 4)
    arrived = lax.all_to_all(coefficients, "tile", split_axis=0, concat_axis=0, tiled=True)
    arrived = arrived.transpose(1, 2, 0, 3, 4).reshape(
        2, rows_local, columns_all, rank_positions, virtual_sources
    )
    receiver_factors = u_factors[0]
    real_arrived, imag_arrived = arrived[0], arrived[1]
    stacked_arrived = jnp.stack(
        [jnp.stack([real_arrived, -imag_arrived]), jnp.stack([imag_arrived, real_arrived])]
    )
    receivers = rows_local * tile_width
    received = (
        jnp.einsum(
            "imdlh,oimdlu->oumh",
            receiver_factors,
            stacked_arrived,
            preferred_element_type=jnp.float32,
        )
        .reshape(1, 2, virtual_sources, receivers)
        .astype(jnp.bfloat16)
    )
    piece = lax.all_gather(received, "freq", axis=0, tiled=True)
    count = piece.shape[0]

    backward = jnp.stack([cosine.T, -sine.T], 2).reshape(time_count, count * 2)
    added = jnp.dot(
        spread_over(backward, virtual_sources),
        piece.reshape(count * 2 * virtual_sources, receivers),
        preferred_element_type=jnp.float32,
    )
    scale_freq = 1.0 / math.sqrt(freq_total)
    return (added * scale_freq).astype(jnp.bfloat16).reshape(time_count, virtual_sources, receivers)


def solution(mesh):
    placed = (
        P("freq", "groups", "tile"),
        P("freq", None, None, "tile", None, None),
        P("freq", None, "tile", None, None, None),
        P("freq", None, "tile"),
    )
    return jax.shard_map(
        per_device,
        mesh=mesh,
        in_specs=placed,
        out_specs=P("freq", "groups", "tile"),
        check_vma=False,
    )
```
